32 devices in a mesh: rows: 16 (over z, y, x), vecs: 2 (over core).
Axes of the slice: x: 2, y: 2, z: 4, core: 2. Of those that a mesh axis runs over, the one named last changes fastest.
Arguments:
- vectors: bfloat16 [8192, 256], P('rows', 'vecs'), may hold values from -6 to 6
- blocks: bfloat16 [64, 32, 128, 128], P('rows'), may hold values from -0.09375 to 0.09375
- scales: float32 [64, 32], P('rows'), may hold values from 0.5 to 1.5
- columns: int32 [64, 32], P('rows'), may hold values from 0 to 63, as said below
- owners: int32 [64], P('rows'), may hold values from 0 to 63, as said below
- center: float32 [1], replicated, may hold values from -0.3 to 0.3
- half_width: float32 [1], replicated, may hold values from 1.5 to 2.5
Outputs:
- filtered: bfloat16 [8192, 256], P('rows', 'vecs')
The draws below stay inside these ranges and needn't reach their ends.
Inputs may be any that keep to these rules, and one draw needn't show every extreme that they name: `columns`: the block rows of one aligned group of 4 block rows read at most one atom of each aligned group of 4 atoms. owners is a permutation of the atoms; the 4 entries of one aligned group of 4 entries lie in distinct aligned groups of 4 atoms.
All inputs are finite; a program needn't handle non-finite values.
Results may differ from the reference program's by a relative error of at most 0.0054.
Values may be sent and summed in bfloat16 or wider, within the bound.
No kernel may reach another device: no remote copies, remote signals or barrier semaphores. Data moves between devices by JAX's collectives and lax.ppermute only.
A program may use at most 64 MiB of HBM per device.

```python
import math
import jax
import jax.numpy as jnp
from jax import lax

B = 128
KBLK = 32
STEPS = 4
ROWB_DEV = 4
ATOMS = 64
ORDER = 8192
VECS = 256


def draw_columns(key, part):
    devices = ATOMS // ROWB_DEV
    picks = jax.random.randint(jax.random.fold_in(key, 11), (devices, devices), 0, ROWB_DEV)
    sources = jax.random.randint(jax.random.fold_in(key, 12), (ATOMS, KBLK), 0, devices)
    device_of = jnp.arange(ATOMS, dtype=jnp.int32) // ROWB_DEV
    chosen = picks[device_of[:, None], sources]
    return (sources * ROWB_DEV + chosen).astype(jnp.int32)


def draw_owners(key, part):
    devices = ATOMS // ROWB_DEV
    offsets = jax.random.permutation(jax.random.fold_in(key, 21), devices)[:ROWB_DEV]
    relabel = jax.random.permutation(jax.random.fold_in(key, 22), devices)
    mapping = jax.random.permutation(jax.random.fold_in(key, 23), devices)
    scores = jax.random.randint(jax.random.fold_in(key, 24), (devices, ROWB_DEV), 0, 1048576)
    scores = scores * ROWB_DEV + jnp.arange(ROWB_DEV, dtype=jnp.int32)[None, :]
    order = jnp.argsort(scores, axis=1).astype(jnp.int32)
    dest = jnp.arange(devices, dtype=jnp.int32)[:, None]
    source = mapping[(relabel[dest] + offsets[order]) % devices]
    return (source * ROWB_DEV + order).reshape(ATOMS).astype(jnp.int32)


def levels(own_key, shape, cuts, smallest, largest):
    loudness, own = 1.0, jax.random.fold_in(own_key, 6)
    for position, blocks in cuts:
        steps = jnp.exp(jax.random.uniform(jax.random.fold_in(own, position), (blocks,), jnp.float32, smallest / len(cuts), largest / len(cuts)))
        loudness = loudness * jnp.repeat(steps, shape[position] // blocks).reshape([-1 if axis == position else 1 for axis in range(len(shape))])
    return loudness


def bell_draw(stream_key, extent, scale, most, shards=(), kind=jnp.bfloat16):
    loudness = levels(stream_key, extent, shards, -0.22, 0.18) if shards else 1.0
    drawn = jax.random.normal(stream_key, extent, jnp.float32) * scale * loudness
    return jnp.minimum(jnp.maximum(drawn, -most), most).astype(kind)


def setup_inputs(seed: int = 0) -> dict:
    splits = jax.random.split(jax.random.key(seed), 8)
    return {
        "vectors": bell_draw(splits[0], (ORDER, VECS), 1.0, 6.0, ((0, 16), (1, 2))),
        "blocks": bell_draw(splits[1], (ATOMS, KBLK, B, B), (KBLK * B) ** -0.5, 0.09375, ((0, 16),)),
        "scales": jnp.clip(jnp.exp(math.log(1.5) - 1.0986123 * jax.random.uniform(splits[2], (ATOMS, KBLK), jnp.float32) ** levels(splits[2], (ATOMS, KBLK), ((0, 16),), -0.2, 0.2)), 0.5, 1.5),
        "columns": draw_columns(jax.random.fold_in(splits[7], 71), 0),
        "owners": draw_owners(jax.random.fold_in(splits[7], 71), 0),
        "center": jnp.clip(jax.random.uniform(splits[5], (1,), jnp.float32, -0.3, 0.3), -0.3, 0.3),
        "half_width": jnp.clip(jax.random.uniform(splits[6], (1,), jnp.float32, 1.5, 2.5), 1.5, 2.5),
    }


def apply_blocks(panels, blocks, scales, columns):
    def one_row(item):
        blk, scl, col = item
        operand = jnp.take(panels, col, axis=0).astype(jnp.float32)
        product = jnp.einsum("kij,kjv->kiv", blk.astype(jnp.float32), operand)
        return jnp.sum(scl[:, None, None] * product, axis=0)
    return lax.map(one_row, (blocks, scales, columns))


def reference(vectors, blocks, scales, columns, owners, center, half_width):
    shift = center[0]
    width = half_width[0]
    previous = vectors.reshape(ATOMS, B, VECS)
    current = ((apply_blocks(previous, blocks, scales, columns) - shift * previous.astype(jnp.float32)) / width).astype(jnp.bfloat16)
    for step in range(STEPS - 1):
        image = apply_blocks(current, blocks, scales, columns)
        upcoming = (2.0 * (image - shift * current.astype(jnp.float32)) / width - previous.astype(jnp.float32)).astype(jnp.bfloat16)
        previous, current = current, upcoming
    placed = jnp.take(current, owners, axis=0)
    return placed.reshape(ORDER, VECS)
```

```python
import jax
import jax.numpy as jnp
from jax import lax
from jax.sharding import PartitionSpec as P

STEPS = 4


def requests(index, nrows, local_rows):
    flat = index.reshape(-1)
    hit = (flat // local_rows)[None, :] == jnp.arange(nrows, dtype=flat.dtype)[:, None]
    return jnp.max(jnp.where(hit, (flat % local_rows)[None, :], 0), axis=1)


def on_device(vectors, blocks, scales, columns, owners, center, half_width):
    nrows = lax.axis_size("rows")
    local_rows = blocks.shape[0]
    per_row = blocks.shape[1]
    orbitals = blocks.shape[2]
    group_width = vectors.shape[1]
    asked = jnp.stack(
        [requests(columns, nrows, local_rows), requests(owners, nrows, local_rows)], axis=1
    )
    granted = lax.all_to_all(asked, "rows", split_axis=0, concat_axis=0, tiled=True)
    wanted = granted[:, 0]
    relay_want = granted[:, 1]
    source_slot = (columns // local_rows).reshape(local_rows * per_row)

    def product(received):
        operand = jnp.take(received, source_slot, axis=0).reshape(
            local_rows, per_row, orbitals, received.shape[2]
        )
        partial_value = jnp.einsum(
            "rkij,rkjv->rkiv", blocks, operand, preferred_element_type=jnp.float32
        )
        return jnp.sum(partial_value * scales[:, :, None, None], axis=1)

    def apply_blocks(panels):
        outgoing = jnp.take(panels, wanted, axis=0)
        received = lax.all_to_all(outgoing, "rows", split_axis=0, concat_axis=0, tiled=True)
        return product(received)

    shift = center[0]
    width = half_width[0]
    previous = vectors.reshape(local_rows, orbitals, group_width)
    current = ((apply_blocks(previous) - shift * previous.astype(jnp.float32)) / width).astype(
        jnp.bfloat16
    )
    for step in range(STEPS - 1):
        image = apply_blocks(current)
        upcoming = (
            2.0 * (image - shift * current.astype(jnp.float32)) / width
            - previous.astype(jnp.float32)
        ).astype(jnp.bfloat16)
        previous, current = (current, upcoming)
    sending = jnp.take(current, relay_want, axis=0)
    arrived = lax.all_to_all(sending, "rows", split_axis=0, concat_axis=0, tiled=True)
    placed = jnp.take(arrived, owners // local_rows, axis=0)
    return placed.reshape(local_rows * orbitals, group_width)


def solution(mesh):
    in_specs = (
        P("rows", "vecs"),
        P("rows", None, None, None),
        P("rows", None),
        P("rows", None),
        P("rows"),
        P(),
        P(),
    )
    out_specs = P("rows", "vecs")
    return jax.shard_map(
        on_device, mesh=mesh, in_specs=in_specs, out_specs=out_specs, check_vma=False
    )
```

```python
import jax
import jax.numpy as jnp
from jax import lax
from jax.sharding import PartitionSpec as P

STEPS = 4


def on_device(vectors, blocks, scales, columns, owners, center, half_width):
    local_rows = blocks.shape[0]
    per_row = blocks.shape[1]
    orbitals = blocks.shape[2]
    group_width = vectors.shape[1]

    def gather_all(panels):
        return lax.all_gather(panels, "rows", axis=0, tiled=True)

    def apply_blocks(panels):
        everything = gather_all(panels)
        operand = jnp.take(everything, columns.reshape(-1), axis=0).reshape(
            local_rows, per_row, orbitals, group_width
        )
        partial_value = jnp.einsum(
            "rkij,rkjv->rkiv", blocks, operand, preferred_element_type=jnp.float32
        )
        return jnp.sum(partial_value * scales[:, :, None, None], axis=1)

    shift = center[0]
    width = half_width[0]
    previous = vectors.reshape(local_rows, orbitals, group_width)
    current = ((apply_blocks(previous) - shift * previous.astype(jnp.float32)) / width).astype(
        jnp.bfloat16
    )
    for step in range(STEPS - 1):
        image = apply_blocks(current)
        upcoming = (
            2.0 * (image - shift * current.astype(jnp.float32)) / width
            - previous.astype(jnp.float32)
        ).astype(jnp.bfloat16)
        previous, current = (current, upcoming)
    placed = jnp.take(gather_all(current), owners, axis=0)
    return placed.reshape(local_rows * orbitals, group_width)


def solution(mesh):
    in_specs = (
        P("rows", "vecs"),
        P("rows", None, None, None),
        P("rows", None),
        P("rows", None),
        P("rows"),
        P(),
        P(),
    )
    out_specs = P("rows", "vecs")
    return jax.shard_map(
        on_device, mesh=mesh, in_specs=in_specs, out_specs=out_specs, check_vma=False
    )
```

```python
import functools

import jax
import jax.numpy as jnp
from jax import lax
from jax.experimental import pallas as pl
from jax.experimental.pallas import tpu as pltpu
from jax.sharding import PartitionSpec as P

STEPS = 4


def requests(index, nrows, local_rows):
    flat = index.reshape(-1)
    hit = (flat // local_rows)[None, :] == jnp.arange(nrows, dtype=flat.dtype)[:, None]
    return jnp.max(jnp.where(hit, (flat % local_rows)[None, :], 0), axis=1)


def step_kernel(first, per_row, slot_ref, scl_ref, sw_ref, recv_ref, blk_ref, cur_ref, *rest):
    if first:
        (out_ref,) = rest
    else:
        prev_ref, out_ref = rest
    r = pl.program_id(0)

    def body(k, acc):
        s = slot_ref[r * per_row + k]
        prod = jnp.dot(blk_ref[0, k], recv_ref[s], preferred_element_type=jnp.float32)
        return acc + scl_ref[r, k] * prod

    acc = lax.fori_loop(
        0, per_row, body, jnp.zeros(out_ref.shape[1:], jnp.float32), unroll=True
    )
    shift = sw_ref[0]
    width = sw_ref[1]
    cur = cur_ref[0].astype(jnp.float32)
    if first:
        new = (acc - shift * cur) / width
    else:
        new = 2.0 * (acc - shift * cur) / width - prev_ref[0].astype(jnp.float32)
    out_ref[0] = new.astype(out_ref.dtype)


def chebyshev_step(slot, scales, sw, received, blocks, cur, prev):
    local_rows, per_row, orbitals, _ = blocks.shape
    width = cur.shape[2]
    first = prev is None
    row_spec = pl.BlockSpec((1, orbitals, width), lambda r, s: (r, 0, 0))
    in_specs = [
        pl.BlockSpec(memory_space=pltpu.SMEM),
        pl.BlockSpec(memory_space=pltpu.SMEM),
        pl.BlockSpec(received.shape, lambda r, s: (0, 0, 0)),
        pl.BlockSpec((1, per_row, orbitals, orbitals), lambda r, s: (r, 0, 0, 0)),
        row_spec,
    ]
    args = [scales, sw, received, blocks, cur]
    if not first:
        in_specs.append(row_spec)
        args.append(prev)
    flops = 2 * local_rows * per_row * orbitals * orbitals * width
    nbytes = blocks.size * 2 + received.size * 2 + 3 * cur.size * 2
    return pl.pallas_call(
        functools.partial(step_kernel, first, per_row),
        out_shape=jax.ShapeDtypeStruct(cur.shape, jnp.bfloat16),
        grid_spec=pltpu.PrefetchScalarGridSpec(
            num_scalar_prefetch=1,
            grid=(local_rows,),
            in_specs=in_specs,
            out_specs=row_spec,
        ),
        cost_estimate=pl.CostEstimate(flops=flops, bytes_accessed=nbytes, transcendentals=0),
    )(slot, *args)


def on_device(vectors, blocks, scales, columns, owners, center, half_width):
    nrows = lax.axis_size("rows")
    local_rows = blocks.shape[0]
    orbitals = blocks.shape[2]
    group_width = vectors.shape[1]
    asked = jnp.stack(
        [requests(columns, nrows, local_rows), requests(owners, nrows, local_rows)], axis=1
    )
    granted = lax.all_to_all(asked, "rows", split_axis=0, concat_axis=0, tiled=True)
    wanted = granted[:, 0]
    relay_want = granted[:, 1]
    slot = (columns // local_rows).reshape(-1)
    sw = jnp.concatenate([center, half_width])

    def exchange(panels):
        outgoing = jnp.take(panels, wanted, axis=0)
        return lax.all_to_all(outgoing, "rows", split_axis=0, concat_axis=0, tiled=True)

    previous = vectors.reshape(local_rows, orbitals, group_width)
    current = chebyshev_step(slot, scales, sw, exchange(previous), blocks, previous, None)
    for step in range(STEPS - 1):
        upcoming = chebyshev_step(slot, scales, sw, exchange(current), blocks, current, previous)
        previous, current = (current, upcoming)
    sending = jnp.take(current, relay_want, axis=0)
    arrived = lax.all_to_all(sending, "rows", split_axis=0, concat_axis=0, tiled=True)
    placed = jnp.take(arrived, owners // local_rows, axis=0)
    return placed.reshape(local_rows * orbitals, group_width)


def solution(mesh):
    in_specs = (
        P("rows", "vecs"),
        P("rows", None, None, None),
        P("rows", None),
        P("rows", None),
        P("rows"),
        P(),
        P(),
    )
    out_specs = P("rows", "vecs")
    return jax.shard_map(
        on_device, mesh=mesh, in_specs=in_specs, out_specs=out_specs, check_vma=False
    )
```

```python
import functools

import jax
import jax.numpy as jnp
from jax import lax
from jax.experimental import pallas as pl
from jax.experimental.pallas import tpu as pltpu
from jax.sharding import PartitionSpec as P

STEPS = 4


def requests(index, nrows, local_rows):
    flat = index.reshape(-1)
    hit = (flat // local_rows)[None, :] == jnp.arange(nrows, dtype=flat.dtype)[:, None]
    return jnp.max(jnp.where(hit, (flat % local_rows)[None, :], 0), axis=1)


def step_kernel(first, cols_ref, pick_ref, scl_ref, c_ref, w_ref, recv_ref, blk_ref, cur_ref, *rest):
    if first:
        out_ref, go_ref, rows_ref = rest
    else:
        prev_ref, out_ref, go_ref, rows_ref = rest
    r = pl.program_id(0)
    local_rows, per_row = cols_ref.shape

    def body(k, acc):
        s = cols_ref[r, k] // local_rows
        prod = jnp.dot(blk_ref[0, k], recv_ref[s], preferred_element_type=jnp.float32)
        return acc + scl_ref[r, k] * prod

    acc = lax.fori_loop(
        0, per_row, body, jnp.zeros(out_ref.shape[1:], jnp.float32), unroll=True
    )
    shift = c_ref[0]
    width = w_ref[0]
    cur = cur_ref[0].astype(jnp.float32)
    if first:
        new = (acc - shift * cur) / width
    else:
        new = 2.0 * (acc - shift * cur) / width - prev_ref[0].astype(jnp.float32)
    new = new.astype(out_ref.dtype)
    out_ref[0] = new
    rows_ref[r] = new

    @pl.when(r == local_rows - 1)
    def _():
        def put(e, carry):
            go_ref[e] = rows_ref[pick_ref[e]]
            return carry

        lax.fori_loop(0, go_ref.shape[0], put, 0)


def chebyshev_step(columns, pick, scales, center, half_width, received, blocks, cur, prev):
    local_rows, per_row, orbitals, _ = blocks.shape
    width = cur.shape[2]
    nrows = pick.shape[0]
    first = prev is None
    row_spec = pl.BlockSpec((1, orbitals, width), lambda r, c, p: (r, 0, 0))
    smem = pl.BlockSpec(memory_space=pltpu.SMEM)
    in_specs = [
        smem,
        smem,
        smem,
        pl.BlockSpec(received.shape, lambda r, c, p: (0, 0, 0)),
        pl.BlockSpec((1, per_row, orbitals, orbitals), lambda r, c, p: (r, 0, 0, 0)),
        row_spec,
    ]
    args = [scales, center, half_width, received, blocks, cur]
    if not first:
        in_specs.append(row_spec)
        args.append(prev)
    flops = 2 * local_rows * per_row * orbitals * orbitals * width
    nbytes = blocks.size * 2 + 2 * received.size * 2 + 3 * cur.size * 2
    return pl.pallas_call(
        functools.partial(step_kernel, first),
        out_shape=(
            jax.ShapeDtypeStruct(cur.shape, jnp.bfloat16),
            jax.ShapeDtypeStruct((nrows, orbitals, width), jnp.bfloat16),
        ),
        grid_spec=pltpu.PrefetchScalarGridSpec(
            num_scalar_prefetch=2,
            grid=(local_rows,),
            in_specs=in_specs,
            out_specs=(row_spec, pl.BlockSpec((nrows, orbitals, width), lambda r, c, p: (0, 0, 0))),
            scratch_shapes=[pltpu.VMEM(cur.shape, jnp.bfloat16)],
        ),
        cost_estimate=pl.CostEstimate(flops=flops, bytes_accessed=nbytes, transcendentals=0),
    )(columns, pick, *args)


def on_device(vectors, blocks, scales, columns, owners, center, half_width):
    nrows = lax.axis_size("rows")
    local_rows = blocks.shape[0]
    orbitals = blocks.shape[2]
    group_width = vectors.shape[1]
    asked = jnp.stack(
        [requests(columns, nrows, local_rows), requests(owners, nrows, local_rows)], axis=1
    )
    granted = lax.all_to_all(asked, "rows", split_axis=0, concat_axis=0, tiled=True)
    wanted = granted[:, 0]
    relay_want = granted[:, 1]

    def exchange(outgoing):
        return lax.all_to_all(outgoing, "rows", split_axis=0, concat_axis=0, tiled=True)

    previous = vectors.reshape(local_rows, orbitals, group_width)
    current, outgoing = chebyshev_step(
        columns, wanted, scales, center, half_width,
        exchange(jnp.take(previous, wanted, axis=0)), blocks, previous, None,
    )
    for step in range(1, STEPS):
        pick = relay_want if step == STEPS - 1 else wanted
        upcoming, outgoing = chebyshev_step(
            columns, pick, scales, center, half_width, exchange(outgoing), blocks, current, previous
        )
        previous, current = (current, upcoming)
    arrived = exchange(outgoing)
    placed = jnp.take(arrived, owners // local_rows, axis=0)
    return placed.reshape(local_rows * orbitals, group_width)


def solution(mesh):
    in_specs = (
        P("rows", "vecs"),
        P("rows", None, None, None),
        P("rows", None),
        P("rows", None),
        P("rows"),
        P(),
        P(),
    )
    out_specs = P("rows", "vecs")
    return jax.shard_map(
        on_device, mesh=mesh, in_specs=in_specs, out_specs=out_specs, check_vma=False
    )
```

```python
import functools

import jax
import jax.numpy as jnp
from jax import lax
from jax.experimental import pallas as pl
from jax.experimental.pallas import tpu as pltpu
from jax.sharding import PartitionSpec as P

STEPS = 4


def requests(index, nrows, local_rows):
    flat = index.reshape(-1)
    hit = (flat // local_rows)[None, :] == jnp.arange(nrows, dtype=flat.dtype)[:, None]
    return jnp.max(jnp.where(hit, (flat % local_rows)[None, :], 0), axis=1)


def step_kernel(first, cols_ref, pick_ref, c_ref, w_ref, recv_ref, blk_ref, cur_ref, *rest):
    if first:
        out_ref, go_ref, rows_ref, stack_ref = rest
    else:
        prev_ref, out_ref, go_ref, rows_ref, stack_ref = rest
    r = pl.program_id(0)
    local_rows, per_row = cols_ref.shape
    orbitals = recv_ref.shape[1]

    def fill(k, carry):
        start = pl.multiple_of(k * orbitals, orbitals)
        stack_ref[pl.ds(start, orbitals), :] = recv_ref[cols_ref[r, k] // local_rows]
        return carry

    lax.fori_loop(0, per_row, fill, 0, unroll=True)
    both = jnp.dot(blk_ref[0], stack_ref[...], preferred_element_type=jnp.float32)
    acc = both[:orbitals] + both[orbitals:]
    shift = c_ref[0]
    width = w_ref[0]
    cur = cur_ref[0].astype(jnp.float32)
    if first:
        new = (acc - shift * cur) / width
    else:
        new = 2.0 * (acc - shift * cur) / width - prev_ref[0].astype(jnp.float32)
    new = new.astype(out_ref.dtype)
    out_ref[0] = new
    rows_ref[r] = new

    @pl.when(r == local_rows - 1)
    def _():
        def put(e, carry):
            go_ref[e] = rows_ref[pick_ref[e]]
            return carry

        lax.fori_loop(0, go_ref.shape[0], put, 0)


def chebyshev_step(columns, pick, center, half_width, received, matrix, cur, prev):
    local_rows, parts, depth = matrix.shape
    orbitals = cur.shape[1]
    width = cur.shape[2]
    nrows = pick.shape[0]
    first = prev is None
    row_spec = pl.BlockSpec((1, orbitals, width), lambda r, c, p: (r, 0, 0))
    smem = pl.BlockSpec(memory_space=pltpu.SMEM)
    in_specs = [
        smem,
        smem,
        pl.BlockSpec(received.shape, lambda r, c, p: (0, 0, 0)),
        pl.BlockSpec((1, parts, depth), lambda r, c, p: (r, 0, 0)),
        row_spec,
    ]
    args = [center, half_width, received, matrix, cur]
    if not first:
        in_specs.append(row_spec)
        args.append(prev)
    flops = 2 * local_rows * parts * depth * width
    nbytes = matrix.size * 2 + 2 * received.size * 2 + 3 * cur.size * 2
    return pl.pallas_call(
        functools.partial(step_kernel, first),
        out_shape=(
            jax.ShapeDtypeStruct(cur.shape, jnp.bfloat16),
            jax.ShapeDtypeStruct((nrows, orbitals, width), jnp.bfloat16),
        ),
        grid_spec=pltpu.PrefetchScalarGridSpec(
            num_scalar_prefetch=2,
            grid=(local_rows,),
            in_specs=in_specs,
            out_specs=(row_spec, pl.BlockSpec((nrows, orbitals, width), lambda r, c, p: (0, 0, 0))),
            scratch_shapes=[
                pltpu.VMEM(cur.shape, jnp.bfloat16),
                pltpu.VMEM((depth, width), jnp.bfloat16),
            ],
        ),
        cost_estimate=pl.CostEstimate(flops=flops, bytes_accessed=nbytes, transcendentals=0),
    )(columns, pick, *args)


def on_device(vectors, blocks, scales, columns, owners, center, half_width):
    nrows = lax.axis_size("rows")
    local_rows = blocks.shape[0]
    orbitals = blocks.shape[2]
    group_width = vectors.shape[1]
    asked = jnp.stack(
        [requests(columns, nrows, local_rows), requests(owners, nrows, local_rows)], axis=1
    )
    granted = lax.all_to_all(asked, "rows", split_axis=0, concat_axis=0, tiled=True)
    wanted = granted[:, 0]
    relay_want = granted[:, 1]

    def exchange(outgoing):
        return lax.all_to_all(outgoing, "rows", split_axis=0, concat_axis=0, tiled=True)

    per_row = blocks.shape[1]
    entries = blocks.astype(jnp.float32) * scales[:, :, None, None]
    high = lax.reduce_precision(entries, exponent_bits=8, mantissa_bits=7)
    low = entries - high
    matrix = (
        jnp.stack([high.astype(jnp.bfloat16), low.astype(jnp.bfloat16)], axis=1)
        .transpose(0, 1, 3, 2, 4)
        .reshape(local_rows, 2 * orbitals, per_row * orbitals)
    )
    previous = vectors.reshape(local_rows, orbitals, group_width)
    current, outgoing = chebyshev_step(
        columns, wanted, center, half_width,
        exchange(jnp.take(previous, wanted, axis=0)), matrix, previous, None,
    )
    for step in range(1, STEPS):
        pick = relay_want if step == STEPS - 1 else wanted
        upcoming, outgoing = chebyshev_step(
            columns, pick, center, half_width, exchange(outgoing), matrix, current, previous
        )
        previous, current = (current, upcoming)
    arrived = exchange(outgoing)
    placed = jnp.take(arrived, owners // local_rows, axis=0)
    return placed.reshape(local_rows * orbitals, group_width)


def solution(mesh):
    in_specs = (
        P("rows", "vecs"),
        P("rows", None, None, None),
        P("rows", None),
        P("rows", None),
        P("rows"),
        P(),
        P(),
    )
    out_specs = P("rows", "vecs")
    return jax.shard_map(
        on_device, mesh=mesh, in_specs=in_specs, out_specs=out_specs, check_vma=False
    )
```

```python
import functools

import jax
import jax.numpy as jnp
from jax import lax
from jax.experimental import pallas as pl
from jax.experimental.pallas import tpu as pltpu
from jax.sharding import PartitionSpec as P

STEPS = 4


def requests_kernel(cols_ref, own_ref, out_ref):
    local_rows, per_row = cols_ref.shape

    def clear(e, carry):
        out_ref[e, 0] = 0
        out_ref[e, 1] = 0
        return carry

    lax.fori_loop(0, out_ref.shape[0], clear, 0)

    def read(i, carry):
        c = cols_ref[i // per_row, i % per_row]
        out_ref[c // local_rows, 0] = c % local_rows
        return carry

    lax.fori_loop(0, local_rows * per_row, read, 0)

    def place(i, carry):
        o = own_ref[i]
        out_ref[o // local_rows, 1] = o % local_rows
        return carry

    lax.fori_loop(0, own_ref.shape[0], place, 0)


def requests(columns, owners, nrows):
    smem = pl.BlockSpec(memory_space=pltpu.SMEM)
    return pl.pallas_call(
        requests_kernel,
        out_shape=jax.ShapeDtypeStruct((nrows, 2), jnp.int32),
        in_specs=[smem, smem],
        out_specs=smem,
    )(columns, owners)


def pick_kernel(which, table_ref, src_ref, out_ref):
    def put(e, carry):
        out_ref[e] = src_ref[table_ref[e, which]]
        return carry

    lax.fori_loop(0, out_ref.shape[0], put, 0)


def pick_rows(table, which, source, count):
    return pl.pallas_call(
        functools.partial(pick_kernel, which),
        out_shape=jax.ShapeDtypeStruct((count,) + source.shape[1:], source.dtype),
        grid_spec=pltpu.PrefetchScalarGridSpec(
            num_scalar_prefetch=1,
            grid=(1,),
            in_specs=[pl.BlockSpec(source.shape, lambda i, t: (0, 0, 0))],
            out_specs=pl.BlockSpec((count,) + source.shape[1:], lambda i, t: (0, 0, 0)),
        ),
    )(table, source)


def step_kernel(first, which, cols_ref, pick_ref, scl_ref, c_ref, w_ref, recv_ref, blk_ref, cur_ref, *rest):
    if first:
        out_ref, go_ref, rows_ref = rest
    else:
        prev_ref, out_ref, go_ref, rows_ref = rest
    r = pl.program_id(0)
    local_rows, per_row = cols_ref.shape

    def body(k, acc):
        s = cols_ref[r, k] // local_rows
        prod = jnp.dot(blk_ref[0, k], recv_ref[s], preferred_element_type=jnp.float32)
        return acc + scl_ref[r, k] * prod

    acc = lax.fori_loop(
        0, per_row, body, jnp.zeros(out_ref.shape[1:], jnp.float32), unroll=True
    )
    shift = c_ref[0]
    width = w_ref[0]
    cur = cur_ref[0].astype(jnp.float32)
    if first:
        new = (acc - shift * cur) / width
    else:
        new = 2.0 * (acc - shift * cur) / width - prev_ref[0].astype(jnp.float32)
    new = new.astype(out_ref.dtype)
    out_ref[0] = new
    rows_ref[r] = new

    @pl.when(r == local_rows - 1)
    def _():
        def put(e, carry):
            go_ref[e] = rows_ref[pick_ref[e, which]]
            return carry

        lax.fori_loop(0, go_ref.shape[0], put, 0)


def chebyshev_step(columns, pick, which, scales, center, half_width, received, blocks, cur, prev):
    local_rows, per_row, orbitals, _ = blocks.shape
    width = cur.shape[2]
    nrows = pick.shape[0]
    first = prev is None
    row_spec = pl.BlockSpec((1, orbitals, width), lambda r, c, p: (r, 0, 0))
    smem = pl.BlockSpec(memory_space=pltpu.SMEM)
    in_specs = [
        smem,
        smem,
        smem,
        pl.BlockSpec(received.shape, lambda r, c, p: (0, 0, 0)),
        pl.BlockSpec((1, per_row, orbitals, orbitals), lambda r, c, p: (r, 0, 0, 0)),
        row_spec,
    ]
    args = [scales, center, half_width, received, blocks, cur]
    if not first:
        in_specs.append(row_spec)
        args.append(prev)
    flops = 2 * local_rows * per_row * orbitals * orbitals * width
    nbytes = blocks.size * 2 + 2 * received.size * 2 + 3 * cur.size * 2
    return pl.pallas_call(
        functools.partial(step_kernel, first, which),
        out_shape=(
            jax.ShapeDtypeStruct(cur.shape, jnp.bfloat16),
            jax.ShapeDtypeStruct((nrows, orbitals, width), jnp.bfloat16),
        ),
        grid_spec=pltpu.PrefetchScalarGridSpec(
            num_scalar_prefetch=2,
            grid=(local_rows,),
            in_specs=in_specs,
            out_specs=(row_spec, pl.BlockSpec((nrows, orbitals, width), lambda r, c, p: (0, 0, 0))),
            scratch_shapes=[pltpu.VMEM(cur.shape, jnp.bfloat16)],
        ),
        cost_estimate=pl.CostEstimate(flops=flops, bytes_accessed=nbytes, transcendentals=0),
    )(columns, pick, *args)


def on_device(vectors, blocks, scales, columns, owners, center, half_width):
    nrows = lax.axis_size("rows")
    local_rows = blocks.shape[0]
    orbitals = blocks.shape[2]
    group_width = vectors.shape[1]
    asked = requests(columns, owners, nrows)
    granted = lax.all_to_all(asked, "rows", split_axis=0, concat_axis=0, tiled=True)

    def exchange(outgoing):
        return lax.all_to_all(outgoing, "rows", split_axis=0, concat_axis=0, tiled=True)

    previous = vectors.reshape(local_rows, orbitals, group_width)
    current, outgoing = chebyshev_step(
        columns, granted, 0, scales, center, half_width,
        exchange(pick_rows(granted, 0, previous, nrows)), blocks, previous, None,
    )
    for step in range(1, STEPS):
        which = 1 if step == STEPS - 1 else 0
        upcoming, outgoing = chebyshev_step(
            columns, granted, which, scales, center, half_width, exchange(outgoing), blocks, current, previous
        )
        previous, current = (current, upcoming)
    arrived = exchange(outgoing)
    placed = pick_rows(
        jnp.stack([owners // local_rows, owners], axis=1), 0, arrived, local_rows
    )
    return placed.reshape(local_rows * orbitals, group_width)


def solution(mesh):
    in_specs = (
        P("rows", "vecs"),
        P("rows", None, None, None),
        P("rows", None),
        P("rows", None),
        P("rows"),
        P(),
        P(),
    )
    out_specs = P("rows", "vecs")
    return jax.shard_map(
        on_device, mesh=mesh, in_specs=in_specs, out_specs=out_specs, check_vma=False
    )
```

```python
import functools

import jax
import jax.numpy as jnp
from jax import lax
from jax.experimental import pallas as pl
from jax.experimental.pallas import tpu as pltpu
from jax.sharding import PartitionSpec as P

STEPS = 4


def requests(index, nrows, local_rows):
    flat = index.reshape(-1)
    hit = (flat // local_rows)[None, :] == jnp.arange(nrows, dtype=flat.dtype)[:, None]
    return jnp.max(jnp.where(hit, (flat % local_rows)[None, :], 0), axis=1)


def step_kernel(first, cols_ref, pick_ref, scl_ref, c_ref, w_ref, recv_ref, blk_ref, cur_ref, *rest):
    if first:
        out_ref, go_ref = rest
    else:
        prev_ref, out_ref, go_ref = rest
    local_rows, per_row = cols_ref.shape
    shift = c_ref[0]
    width = w_ref[0]
    for r in range(local_rows):

        def body(k, acc):
            s = cols_ref[r, k] // local_rows
            prod = jnp.dot(blk_ref[r, k], recv_ref[s], preferred_element_type=jnp.float32)
            return acc + scl_ref[r, k] * prod

        acc = lax.fori_loop(
            0, per_row, body, jnp.zeros(out_ref.shape[1:], jnp.float32), unroll=True
        )
        cur = cur_ref[r].astype(jnp.float32)
        if first:
            new = (acc - shift * cur) / width
        else:
            new = 2.0 * (acc - shift * cur) / width - prev_ref[r].astype(jnp.float32)
        out_ref[r] = new.astype(out_ref.dtype)

    def put(e, carry):
        go_ref[e] = out_ref[pick_ref[e]]
        return carry

    lax.fori_loop(0, go_ref.shape[0], put, 0)


def chebyshev_step(columns, pick, scales, center, half_width, received, blocks, cur, prev):
    local_rows, per_row, orbitals, _ = blocks.shape
    width = cur.shape[2]
    nrows = pick.shape[0]
    first = prev is None
    smem = pl.BlockSpec(memory_space=pltpu.SMEM)
    vmem = pl.BlockSpec(memory_space=pltpu.VMEM)
    args = [columns, pick, scales, center, half_width, received, blocks, cur]
    if not first:
        args.append(prev)
    flops = 2 * local_rows * per_row * orbitals * orbitals * width
    nbytes = blocks.size * 2 + 2 * received.size * 2 + 3 * cur.size * 2
    return pl.pallas_call(
        functools.partial(step_kernel, first),
        out_shape=(
            jax.ShapeDtypeStruct(cur.shape, jnp.bfloat16),
            jax.ShapeDtypeStruct((nrows, orbitals, width), jnp.bfloat16),
        ),
        in_specs=[smem] * 5 + [vmem] * (len(args) - 5),
        out_specs=(vmem, vmem),
        compiler_params=pltpu.CompilerParams(vmem_limit_bytes=8 * 1024 * 1024),
        cost_estimate=pl.CostEstimate(flops=flops, bytes_accessed=nbytes, transcendentals=0),
    )(*args)


def on_device(vectors, blocks, scales, columns, owners, center, half_width):
    nrows = lax.axis_size("rows")
    local_rows = blocks.shape[0]
    orbitals = blocks.shape[2]
    group_width = vectors.shape[1]
    asked = jnp.stack(
        [requests(columns, nrows, local_rows), requests(owners, nrows, local_rows)], axis=1
    )
    granted = lax.all_to_all(asked, "rows", split_axis=0, concat_axis=0, tiled=True)
    wanted = granted[:, 0]
    relay_want = granted[:, 1]

    def exchange(outgoing):
        return lax.all_to_all(outgoing, "rows", split_axis=0, concat_axis=0, tiled=True)

    blocks = pltpu.with_memory_space_constraint(blocks, pltpu.VMEM)
    previous = vectors.reshape(local_rows, orbitals, group_width)
    current, outgoing = chebyshev_step(
        columns, wanted, scales, center, half_width,
        exchange(jnp.take(previous, wanted, axis=0)), blocks, previous, None,
    )
    for step in range(1, STEPS):
        pick = relay_want if step == STEPS - 1 else wanted
        upcoming, outgoing = chebyshev_step(
            columns, pick, scales, center, half_width, exchange(outgoing), blocks, current, previous
        )
        previous, current = (current, upcoming)
    arrived = exchange(outgoing)
    placed = jnp.take(arrived, owners // local_rows, axis=0)
    return placed.reshape(local_rows * orbitals, group_width)


def solution(mesh):
    in_specs = (
        P("rows", "vecs"),
        P("rows", None, None, None),
        P("rows", None),
        P("rows", None),
        P("rows"),
        P(),
        P(),
    )
    out_specs = P("rows", "vecs")
    return jax.shard_map(
        on_device, mesh=mesh, in_specs=in_specs, out_specs=out_specs, check_vma=False
    )
```

```python
import functools

import jax
import jax.numpy as jnp
from jax import lax
from jax.experimental import pallas as pl
from jax.experimental.pallas import tpu as pltpu
from jax.sharding import PartitionSpec as P

STEPS = 4


def requests(index, nrows, local_rows):
    devices = jnp.arange(nrows, dtype=index.dtype).reshape((nrows,) + (1,) * index.ndim)
    hit = (index // local_rows)[None] == devices
    return jnp.max(jnp.where(hit, (index % local_rows)[None], 0), axis=tuple(range(1, index.ndim + 1)))


def step_kernel(first, cols_ref, pick_ref, scl_ref, c_ref, w_ref, recv_ref, blk_ref, cur_ref, *rest):
    if first:
        out_ref, go_ref = rest
    else:
        prev_ref, out_ref, go_ref = rest
    local_rows, per_row = cols_ref.shape
    shift = c_ref[0]
    width = w_ref[0]
    for r in range(local_rows):

        def body(k, acc):
            s = cols_ref[r, k] // local_rows
            prod = jnp.dot(blk_ref[r, k], recv_ref[s], preferred_element_type=jnp.float32)
            return acc + scl_ref[r, k] * prod

        acc = lax.fori_loop(
            0, per_row, body, jnp.zeros(out_ref.shape[1:], jnp.float32), unroll=True
        )
        cur = cur_ref[r].astype(jnp.float32)
        if first:
            new = (acc - shift * cur) / width
        else:
            new = 2.0 * (acc - shift * cur) / width - prev_ref[r].astype(jnp.float32)
        out_ref[r] = new.astype(out_ref.dtype)

    def put(e, carry):
        go_ref[e] = out_ref[pick_ref[e]]
        return carry

    lax.fori_loop(0, go_ref.shape[0], put, 0)


def chebyshev_step(columns, pick, scales, center, half_width, received, blocks, cur, prev):
    local_rows, per_row, orbitals, _ = blocks.shape
    width = cur.shape[2]
    nrows = pick.shape[0]
    first = prev is None
    smem = pl.BlockSpec(memory_space=pltpu.SMEM)
    vmem = pl.BlockSpec(memory_space=pltpu.VMEM)
    args = [columns, pick, scales, center, half_width, received, blocks, cur]
    if not first:
        args.append(prev)
    flops = 2 * local_rows * per_row * orbitals * orbitals * width
    nbytes = blocks.size * 2 + 2 * received.size * 2 + 3 * cur.size * 2
    return pl.pallas_call(
        functools.partial(step_kernel, first),
        out_shape=(
            jax.ShapeDtypeStruct(cur.shape, jnp.bfloat16),
            jax.ShapeDtypeStruct((nrows, orbitals, width), jnp.bfloat16),
        ),
        in_specs=[smem] * 5 + [vmem] * (len(args) - 5),
        out_specs=(vmem, vmem),
        compiler_params=pltpu.CompilerParams(vmem_limit_bytes=8 * 1024 * 1024),
        cost_estimate=pl.CostEstimate(flops=flops, bytes_accessed=nbytes, transcendentals=0),
    )(*args)


def on_device(vectors, blocks, scales, columns, owners, center, half_width):
    nrows = lax.axis_size("rows")
    local_rows = blocks.shape[0]
    orbitals = blocks.shape[2]
    group_width = vectors.shape[1]
    asked = jnp.stack(
        [requests(columns, nrows, local_rows), requests(owners, nrows, local_rows)], axis=1
    )
    granted = lax.all_to_all(asked, "rows", split_axis=0, concat_axis=0, tiled=True)
    wanted = granted[:, 0]
    relay_want = granted[:, 1]

    def exchange(outgoing):
        return lax.all_to_all(outgoing, "rows", split_axis=0, concat_axis=0, tiled=True)

    blocks = pltpu.with_memory_space_constraint(blocks, pltpu.VMEM)
    previous = vectors.reshape(local_rows, orbitals, group_width)
    current, outgoing = chebyshev_step(
        columns, wanted, scales, center, half_width,
        exchange(jnp.take(previous, wanted, axis=0, mode="clip")), blocks, previous, None,
    )
    for step in range(1, STEPS):
        pick = relay_want if step == STEPS - 1 else wanted
        upcoming, outgoing = chebyshev_step(
            columns, pick, scales, center, half_width, exchange(outgoing), blocks, current, previous
        )
        previous, current = (current, upcoming)
    arrived = exchange(outgoing)
    placed = jnp.take(arrived, owners // local_rows, axis=0, mode="clip")
    return placed.reshape(local_rows * orbitals, group_width)


def solution(mesh):
    in_specs = (
        P("rows", "vecs"),
        P("rows", None, None, None),
        P("rows", None),
        P("rows", None),
        P("rows"),
        P(),
        P(),
    )
    out_specs = P("rows", "vecs")
    return jax.shard_map(
        on_device, mesh=mesh, in_specs=in_specs, out_specs=out_specs, check_vma=False
    )
```

```python
import functools

import jax
import jax.numpy as jnp
from jax import lax
from jax.experimental import pallas as pl
from jax.experimental.pallas import tpu as pltpu
from jax.sharding import PartitionSpec as P

STEPS = 4


def requests(index, nrows, local_rows):
    devices = jnp.arange(nrows, dtype=index.dtype).reshape((nrows,) + (1,) * index.ndim)
    hit = (index // local_rows)[None] == devices
    return jnp.max(jnp.where(hit, (index % local_rows)[None], 0), axis=tuple(range(1, index.ndim + 1)))


def step_kernel(first, cols_ref, pick_ref, scl_ref, c_ref, w_ref, recv_ref, blk_ref, cur_ref, *rest):
    if first:
        out_ref, go_ref = rest
    else:
        prev_ref, out_ref, go_ref = rest
    local_rows, per_row = cols_ref.shape
    shift = c_ref[0]
    width = w_ref[0]
    for r in range(local_rows):

        def body(k, acc):
            s = cols_ref[r, k] // local_rows
            prod = jnp.dot(blk_ref[r, k], recv_ref[s], preferred_element_type=jnp.float32)
            return acc + scl_ref[r, k] * prod

        acc = lax.fori_loop(
            0, per_row, body, jnp.zeros(out_ref.shape[1:], jnp.float32), unroll=True
        )
        cur = cur_ref[r].astype(jnp.float32)
        if first:
            new = (acc - shift * cur) / width
        else:
            new = 2.0 * (acc - shift * cur) / width - prev_ref[r].astype(jnp.float32)
        out_ref[r] = new.astype(out_ref.dtype)

    def put(e, carry):
        go_ref[e] = out_ref[pick_ref[e]]
        return carry

    lax.fori_loop(0, go_ref.shape[0], put, 0)


def chebyshev_step(columns, pick, scales, center, half_width, received, blocks, cur, prev):
    local_rows, per_row, orbitals, _ = blocks.shape
    width = cur.shape[2]
    nrows = pick.shape[0]
    first = prev is None
    smem = pl.BlockSpec(memory_space=pltpu.SMEM)
    vmem = pl.BlockSpec(memory_space=pltpu.VMEM)
    args = [columns, pick, scales, center, half_width, received, blocks, cur]
    if not first:
        args.append(prev)
    flops = 2 * local_rows * per_row * orbitals * orbitals * width
    nbytes = blocks.size * 2 + 2 * received.size * 2 + 3 * cur.size * 2
    return pl.pallas_call(
        functools.partial(step_kernel, first),
        out_shape=(
            jax.ShapeDtypeStruct(cur.shape, jnp.bfloat16),
            jax.ShapeDtypeStruct((nrows, orbitals, width), jnp.bfloat16),
        ),
        in_specs=[smem] * 5 + [vmem] * (len(args) - 5),
        out_specs=(vmem, vmem),
        compiler_params=pltpu.CompilerParams(vmem_limit_bytes=8 * 1024 * 1024),
        cost_estimate=pl.CostEstimate(flops=flops, bytes_accessed=nbytes, transcendentals=0),
    )(*args)


def select_rows(panels, index):
    chosen = jnp.broadcast_to(panels[0][None], (index.shape[0],) + panels.shape[1:])
    for atom in range(1, panels.shape[0]):
        chosen = jnp.where((index == atom)[:, None, None], panels[atom][None], chosen)
    return chosen


def on_device(vectors, blocks, scales, columns, owners, center, half_width):
    nrows = lax.axis_size("rows")
    local_rows = blocks.shape[0]
    orbitals = blocks.shape[2]
    group_width = vectors.shape[1]
    asked = jnp.stack(
        [requests(columns, nrows, local_rows), requests(owners, nrows, local_rows)], axis=1
    )
    granted = lax.all_to_all(asked, "rows", split_axis=0, concat_axis=0, tiled=True)
    wanted = granted[:, 0]
    relay_want = granted[:, 1]

    def exchange(outgoing):
        return lax.all_to_all(outgoing, "rows", split_axis=0, concat_axis=0, tiled=True)

    blocks = pltpu.with_memory_space_constraint(blocks, pltpu.VMEM)
    previous = vectors.reshape(local_rows, orbitals, group_width)
    current, outgoing = chebyshev_step(
        columns, wanted, scales, center, half_width,
        exchange(select_rows(previous, wanted)), blocks, previous, None,
    )
    for step in range(1, STEPS):
        pick = relay_want if step == STEPS - 1 else wanted
        upcoming, outgoing = chebyshev_step(
            columns, pick, scales, center, half_width, exchange(outgoing), blocks, current, previous
        )
        previous, current = (current, upcoming)
    arrived = exchange(outgoing)
    placed = jnp.take(arrived, owners // local_rows, axis=0, mode="clip")
    return placed.reshape(local_rows * orbitals, group_width)


def solution(mesh):
    in_specs = (
        P("rows", "vecs"),
        P("rows", None, None, None),
        P("rows", None),
        P("rows", None),
        P("rows"),
        P(),
        P(),
    )
    out_specs = P("rows", "vecs")
    return jax.shard_map(
        on_device, mesh=mesh, in_specs=in_specs, out_specs=out_specs, check_vma=False
    )
```

```python
import functools

import jax
import jax.numpy as jnp
from jax import lax
from jax.experimental import pallas as pl
from jax.experimental.pallas import tpu as pltpu
from jax.sharding import PartitionSpec as P

STEPS = 4


def requests(index, nrows, local_rows):
    devices = jnp.arange(nrows, dtype=index.dtype).reshape((nrows,) + (1,) * index.ndim)
    hit = (index // local_rows)[None] == devices
    return jnp.max(jnp.where(hit, (index % local_rows)[None], 0), axis=tuple(range(1, index.ndim + 1)))


def step_kernel(first, cols_hbm, pick_ref, scl_hbm, c_ref, w_ref, recv_ref, blk_ref, cur_hbm, *rest):
    if first:
        out_ref, go_ref, cols_ref, scl_ref, cur_ref, sems = rest
    else:
        prev_ref, out_ref, go_ref, cols_ref, scl_ref, cur_ref, sems = rest
    copies = [
        pltpu.make_async_copy(cols_hbm, cols_ref, sems.at[0]),
        pltpu.make_async_copy(scl_hbm, scl_ref, sems.at[1]),
        pltpu.make_async_copy(cur_hbm, cur_ref, sems.at[2]),
    ]
    for copy in copies:
        copy.start()
    copies[0].wait()
    copies[1].wait()
    local_rows, per_row = cols_ref.shape
    shift = c_ref[0]
    width = w_ref[0]
    for r in range(local_rows):

        def body(k, acc):
            s = cols_ref[r, k] // local_rows
            prod = jnp.dot(blk_ref[r, k], recv_ref[s], preferred_element_type=jnp.float32)
            return acc + scl_ref[r, k] * prod

        acc = lax.fori_loop(
            0, per_row, body, jnp.zeros(out_ref.shape[1:], jnp.float32), unroll=True
        )
        if r == 0:
            copies[2].wait()
        cur = cur_ref[r].astype(jnp.float32)
        if first:
            new = (acc - shift * cur) / width
        else:
            new = 2.0 * (acc - shift * cur) / width - prev_ref[r].astype(jnp.float32)
        out_ref[r] = new.astype(out_ref.dtype)

    def put(e, carry):
        go_ref[e] = out_ref[pick_ref[e]]
        return carry

    lax.fori_loop(0, go_ref.shape[0], put, 0)


def chebyshev_step(columns, pick, scales, center, half_width, received, blocks, cur, prev):
    local_rows, per_row, orbitals, _ = blocks.shape
    width = cur.shape[2]
    nrows = pick.shape[0]
    first = prev is None
    smem = pl.BlockSpec(memory_space=pltpu.SMEM)
    vmem = pl.BlockSpec(memory_space=pltpu.VMEM)
    anywhere = pl.BlockSpec(memory_space=pl.ANY)
    hbm = pltpu.MemorySpace.HBM
    if first:
        cur = pltpu.with_memory_space_constraint(cur, hbm)
    args = [
        pltpu.with_memory_space_constraint(columns, hbm), pick,
        pltpu.with_memory_space_constraint(scales, hbm), center, half_width, received, blocks, cur,
    ]
    in_specs = [anywhere, smem, anywhere, smem, smem, vmem, vmem, anywhere]
    if not first:
        args.append(prev)
        in_specs.append(vmem)
    flops = 2 * local_rows * per_row * orbitals * orbitals * width
    nbytes = blocks.size * 2 + 2 * received.size * 2 + 3 * cur.size * 2
    return pl.pallas_call(
        functools.partial(step_kernel, first),
        out_shape=(
            jax.ShapeDtypeStruct(cur.shape, jnp.bfloat16),
            jax.ShapeDtypeStruct((nrows, orbitals, width), jnp.bfloat16),
        ),
        in_specs=in_specs,
        out_specs=(vmem, vmem),
        scratch_shapes=[
            pltpu.SMEM(columns.shape, columns.dtype),
            pltpu.SMEM(scales.shape, scales.dtype),
            pltpu.VMEM(cur.shape, cur.dtype),
            pltpu.SemaphoreType.DMA((3,)),
        ],
        compiler_params=pltpu.CompilerParams(vmem_limit_bytes=8 * 1024 * 1024),
        cost_estimate=pl.CostEstimate(flops=flops, bytes_accessed=nbytes, transcendentals=0),
    )(*args)


def select_rows(panels, index):
    chosen = jnp.broadcast_to(panels[0][None], (index.shape[0],) + panels.shape[1:])
    for atom in range(1, panels.shape[0]):
        chosen = jnp.where((index == atom)[:, None, None], panels[atom][None], chosen)
    return chosen


def on_device(vectors, blocks, scales, columns, owners, center, half_width):
    nrows = lax.axis_size("rows")
    local_rows = blocks.shape[0]
    orbitals = blocks.shape[2]
    group_width = vectors.shape[1]
    asked = jnp.stack(
        [requests(columns, nrows, local_rows), requests(owners, nrows, local_rows)], axis=1
    )
    granted = lax.all_to_all(asked, "rows", split_axis=0, concat_axis=0, tiled=True)
    wanted = granted[:, 0]
    relay_want = granted[:, 1]

    def exchange(outgoing):
        return lax.all_to_all(outgoing, "rows", split_axis=0, concat_axis=0, tiled=True)

    blocks = pltpu.with_memory_space_constraint(blocks, pltpu.VMEM)
    previous = vectors.reshape(local_rows, orbitals, group_width)
    current, outgoing = chebyshev_step(
        columns, wanted, scales, center, half_width,
        exchange(select_rows(previous, wanted)), blocks, previous, None,
    )
    for step in range(1, STEPS):
        pick = relay_want if step == STEPS - 1 else wanted
        upcoming, outgoing = chebyshev_step(
            columns, pick, scales, center, half_width, exchange(outgoing), blocks, current, previous
        )
        previous, current = (current, upcoming)
    arrived = exchange(outgoing)
    placed = jnp.take(arrived, owners // local_rows, axis=0, mode="clip")
    return placed.reshape(local_rows * orbitals, group_width)


def solution(mesh):
    in_specs = (
        P("rows", "vecs"),
        P("rows", None, None, None),
        P("rows", None),
        P("rows", None),
        P("rows"),
        P(),
        P(),
    )
    out_specs = P("rows", "vecs")
    return jax.shard_map(
        on_device, mesh=mesh, in_specs=in_specs, out_specs=out_specs, check_vma=False
    )
```

```python
import functools

import jax
import jax.numpy as jnp
from jax import lax
from jax.experimental import pallas as pl
from jax.experimental.pallas import tpu as pltpu
from jax.sharding import PartitionSpec as P

STEPS = 4


def requests(index, nrows, local_rows):
    devices = jnp.arange(nrows, dtype=index.dtype).reshape((nrows,) + (1,) * index.ndim)
    hit = (index // local_rows)[None] == devices
    return jnp.max(jnp.where(hit, (index % local_rows)[None], 0), axis=tuple(range(1, index.ndim + 1)))


def step_kernel(first, cols_ref, pick_ref, scl_ref, c_ref, w_ref, recv_ref, blk_ref, cur_ref, *rest):
    if first:
        out_ref, go_ref = rest
    else:
        prev_ref, out_ref, go_ref = rest
    local_rows, per_row = cols_ref.shape
    shift = c_ref[0]
    width = w_ref[0]
    for r in range(local_rows):

        def body(k, acc):
            s = cols_ref[r, k] // local_rows
            prod = jnp.dot(blk_ref[r, k], recv_ref[s], preferred_element_type=jnp.float32)
            return acc + scl_ref[r, k] * prod

        acc = lax.fori_loop(
            0, per_row, body, jnp.zeros(out_ref.shape[1:], jnp.float32), unroll=True
        )
        cur = cur_ref[r].astype(jnp.float32)
        if first:
            new = (acc - shift * cur) / width
        else:
            new = 2.0 * (acc - shift * cur) / width - prev_ref[r].astype(jnp.float32)
        out_ref[r] = new.astype(out_ref.dtype)

    def put(e, carry):
        go_ref[e] = out_ref[pick_ref[e]]
        return carry

    lax.fori_loop(0, go_ref.shape[0], put, 0)


def first_step_kernel(first, cols_hbm, pick_ref, scl_hbm, c_ref, w_ref, recv_ref, blk_ref, cur_hbm, *rest):
    if first:
        out_ref, go_ref, cols_ref, scl_ref, cur_ref, sems = rest
    else:
        prev_ref, out_ref, go_ref, cols_ref, scl_ref, cur_ref, sems = rest
    copies = [
        pltpu.make_async_copy(cols_hbm, cols_ref, sems.at[0]),
        pltpu.make_async_copy(scl_hbm, scl_ref, sems.at[1]),
        pltpu.make_async_copy(cur_hbm, cur_ref, sems.at[2]),
    ]
    for copy in copies:
        copy.start()
    copies[0].wait()
    copies[1].wait()
    local_rows, per_row = cols_ref.shape
    shift = c_ref[0]
    width = w_ref[0]
    for r in range(local_rows):

        def body(k, acc):
            s = cols_ref[r, k] // local_rows
            prod = jnp.dot(blk_ref[r, k], recv_ref[s], preferred_element_type=jnp.float32)
            return acc + scl_ref[r, k] * prod

        acc = lax.fori_loop(
            0, per_row, body, jnp.zeros(out_ref.shape[1:], jnp.float32), unroll=True
        )
        if r == 0:
            copies[2].wait()
        cur = cur_ref[r].astype(jnp.float32)
        if first:
            new = (acc - shift * cur) / width
        else:
            new = 2.0 * (acc - shift * cur) / width - prev_ref[r].astype(jnp.float32)
        out_ref[r] = new.astype(out_ref.dtype)

    def put(e, carry):
        go_ref[e] = out_ref[pick_ref[e]]
        return carry

    lax.fori_loop(0, go_ref.shape[0], put, 0)


def chebyshev_step(columns, pick, scales, center, half_width, received, blocks, cur, prev):
    local_rows, per_row, orbitals, _ = blocks.shape
    width = cur.shape[2]
    nrows = pick.shape[0]
    first = prev is None
    smem = pl.BlockSpec(memory_space=pltpu.SMEM)
    vmem = pl.BlockSpec(memory_space=pltpu.VMEM)
    args = [columns, pick, scales, center, half_width, received, blocks, cur]
    if not first:
        args.append(prev)
    flops = 2 * local_rows * per_row * orbitals * orbitals * width
    nbytes = blocks.size * 2 + 2 * received.size * 2 + 3 * cur.size * 2
    return pl.pallas_call(
        functools.partial(step_kernel, first),
        out_shape=(
            jax.ShapeDtypeStruct(cur.shape, jnp.bfloat16),
            jax.ShapeDtypeStruct((nrows, orbitals, width), jnp.bfloat16),
        ),
        in_specs=[smem] * 5 + [vmem] * (len(args) - 5),
        out_specs=(vmem, vmem),
        compiler_params=pltpu.CompilerParams(vmem_limit_bytes=8 * 1024 * 1024),
        cost_estimate=pl.CostEstimate(flops=flops, bytes_accessed=nbytes, transcendentals=0),
    )(*args)


def first_chebyshev_step(columns, pick, scales, center, half_width, received, blocks, cur, prev):
    local_rows, per_row, orbitals, _ = blocks.shape
    width = cur.shape[2]
    nrows = pick.shape[0]
    first = prev is None
    smem = pl.BlockSpec(memory_space=pltpu.SMEM)
    vmem = pl.BlockSpec(memory_space=pltpu.VMEM)
    anywhere = pl.BlockSpec(memory_space=pl.ANY)
    hbm = pltpu.MemorySpace.HBM
    if first:
        cur = pltpu.with_memory_space_constraint(cur, hbm)
    args = [
        pltpu.with_memory_space_constraint(columns, hbm), pick,
        pltpu.with_memory_space_constraint(scales, hbm), center, half_width, received, blocks, cur,
    ]
    in_specs = [anywhere, smem, anywhere, smem, smem, vmem, vmem, anywhere]
    if not first:
        args.append(prev)
        in_specs.append(vmem)
    flops = 2 * local_rows * per_row * orbitals * orbitals * width
    nbytes = blocks.size * 2 + 2 * received.size * 2 + 3 * cur.size * 2
    return pl.pallas_call(
        functools.partial(first_step_kernel, first),
        out_shape=(
            jax.ShapeDtypeStruct(cur.shape, jnp.bfloat16),
            jax.ShapeDtypeStruct((nrows, orbitals, width), jnp.bfloat16),
        ),
        in_specs=in_specs,
        out_specs=(vmem, vmem),
        scratch_shapes=[
            pltpu.SMEM(columns.shape, columns.dtype),
            pltpu.SMEM(scales.shape, scales.dtype),
            pltpu.VMEM(cur.shape, cur.dtype),
            pltpu.SemaphoreType.DMA((3,)),
        ],
        compiler_params=pltpu.CompilerParams(vmem_limit_bytes=8 * 1024 * 1024),
        cost_estimate=pl.CostEstimate(flops=flops, bytes_accessed=nbytes, transcendentals=0),
    )(*args)


def select_rows(panels, index):
    chosen = jnp.broadcast_to(panels[0][None], (index.shape[0],) + panels.shape[1:])
    for atom in range(1, panels.shape[0]):
        chosen = jnp.where((index == atom)[:, None, None], panels[atom][None], chosen)
    return chosen


def on_device(vectors, blocks, scales, columns, owners, center, half_width):
    nrows = lax.axis_size("rows")
    local_rows = blocks.shape[0]
    orbitals = blocks.shape[2]
    group_width = vectors.shape[1]
    asked = jnp.stack(
        [requests(columns, nrows, local_rows), requests(owners, nrows, local_rows)], axis=1
    )
    granted = lax.all_to_all(asked, "rows", split_axis=0, concat_axis=0, tiled=True)
    wanted = granted[:, 0]
    relay_want = granted[:, 1]

    def exchange(outgoing):
        return lax.all_to_all(outgoing, "rows", split_axis=0, concat_axis=0, tiled=True)

    blocks = pltpu.with_memory_space_constraint(blocks, pltpu.VMEM)
    previous = vectors.reshape(local_rows, orbitals, group_width)
    current, outgoing = first_chebyshev_step(
        columns, wanted, scales, center, half_width,
        exchange(select_rows(previous, wanted)), blocks, previous, None,
    )
    for step in range(1, STEPS):
        pick = relay_want if step == STEPS - 1 else wanted
        upcoming, outgoing = chebyshev_step(
            columns, pick, scales, center, half_width, exchange(outgoing), blocks, current, previous
        )
        previous, current = (current, upcoming)
    arrived = exchange(outgoing)
    placed = jnp.take(arrived, owners // local_rows, axis=0, mode="clip")
    return placed.reshape(local_rows * orbitals, group_width)


def solution(mesh):
    in_specs = (
        P("rows", "vecs"),
        P("rows", None, None, None),
        P("rows", None),
        P("rows", None),
        P("rows"),
        P(),
        P(),
    )
    out_specs = P("rows", "vecs")
    return jax.shard_map(
        on_device, mesh=mesh, in_specs=in_specs, out_specs=out_specs, check_vma=False
    )
```

```python
import functools

import jax
import jax.numpy as jnp
from jax import lax
from jax.experimental import pallas as pl
from jax.experimental.pallas import tpu as pltpu
from jax.sharding import PartitionSpec as P

STEPS = 4


def requests(index, nrows, local_rows):
    devices = jnp.arange(nrows, dtype=index.dtype).reshape((nrows,) + (1,) * index.ndim)
    hit = (index // local_rows)[None] == devices
    return jnp.max(jnp.where(hit, (index % local_rows)[None], 0), axis=tuple(range(1, index.ndim + 1)))


def step_kernel(first, cols_ref, pick_ref, scl_ref, c_ref, w_ref, recv_ref, blk_ref, cur_ref, *rest):
    if first:
        out_ref, go_ref = rest
    else:
        prev_ref, out_ref, go_ref = rest
    local_rows, per_row = cols_ref.shape
    shift = c_ref[0]
    width = w_ref[0]
    for r in range(local_rows):

        def body(k, acc):
            s = cols_ref[r, k] // local_rows
            prod = jnp.dot(blk_ref[r, k], recv_ref[s], preferred_element_type=jnp.float32)
            return acc + scl_ref[r, k] * prod

        acc = lax.fori_loop(
            0, per_row, body, jnp.zeros(out_ref.shape[1:], jnp.float32), unroll=True
        )
        cur = cur_ref[r].astype(jnp.float32)
        if first:
            new = (acc - shift * cur) / width
        else:
            new = 2.0 * (acc - shift * cur) / width - prev_ref[r].astype(jnp.float32)
        out_ref[r] = new.astype(out_ref.dtype)

    def put(e, carry):
        go_ref[e] = out_ref[pick_ref[e]]
        return carry

    lax.fori_loop(0, go_ref.shape[0], put, 0)


def first_step_kernel(first, cols_hbm, pick_ref, scl_hbm, c_ref, w_ref, recv_ref, blk_ref, cur_hbm, *rest):
    if first:
        out_ref, go_ref, cols_ref, scl_ref, cur_ref, sems = rest
    else:
        prev_ref, out_ref, go_ref, cols_ref, scl_ref, cur_ref, sems = rest
    copies = [
        pltpu.make_async_copy(cols_hbm, cols_ref, sems.at[0]),
        pltpu.make_async_copy(scl_hbm, scl_ref, sems.at[1]),
        pltpu.make_async_copy(cur_hbm, cur_ref, sems.at[2]),
    ]
    for copy in copies:
        copy.start()
    copies[0].wait()
    copies[1].wait()
    local_rows, per_row = cols_ref.shape
    shift = c_ref[0]
    width = w_ref[0]
    for r in range(local_rows):

        def body(k, acc):
            s = cols_ref[r, k] // local_rows
            prod = jnp.dot(blk_ref[r, k], recv_ref[s], preferred_element_type=jnp.float32)
            return acc + scl_ref[r, k] * prod

        acc = lax.fori_loop(
            0, per_row, body, jnp.zeros(out_ref.shape[1:], jnp.float32), unroll=True
        )
        if r == 0:
            copies[2].wait()
        cur = cur_ref[r].astype(jnp.float32)
        if first:
            new = (acc - shift * cur) / width
        else:
            new = 2.0 * (acc - shift * cur) / width - prev_ref[r].astype(jnp.float32)
        out_ref[r] = new.astype(out_ref.dtype)

    def put(e, carry):
        go_ref[e] = out_ref[pick_ref[e]]
        return carry

    lax.fori_loop(0, go_ref.shape[0], put, 0)


def chebyshev_step(columns, pick, scales, center, half_width, received, blocks, cur, prev):
    local_rows, per_row, orbitals, _ = blocks.shape
    width = cur.shape[2]
    nrows = pick.shape[0]
    first = prev is None
    smem = pl.BlockSpec(memory_space=pltpu.SMEM)
    vmem = pl.BlockSpec(memory_space=pltpu.VMEM)
    args = [columns, pick, scales, center, half_width, received, blocks, cur]
    if not first:
        args.append(prev)
    flops = 2 * local_rows * per_row * orbitals * orbitals * width
    nbytes = blocks.size * 2 + 2 * received.size * 2 + 3 * cur.size * 2
    return pl.pallas_call(
        functools.partial(step_kernel, first),
        out_shape=(
            jax.ShapeDtypeStruct(cur.shape, jnp.bfloat16),
            jax.ShapeDtypeStruct((nrows, orbitals, width), jnp.bfloat16),
        ),
        in_specs=[smem] * 5 + [vmem] * (len(args) - 5),
        out_specs=(vmem, vmem),
        compiler_params=pltpu.CompilerParams(vmem_limit_bytes=8 * 1024 * 1024),
        cost_estimate=pl.CostEstimate(flops=flops, bytes_accessed=nbytes, transcendentals=0),
    )(*args)


def first_chebyshev_step(columns, pick, scales, center, half_width, received, blocks, cur, prev):
    local_rows, per_row, orbitals, _ = blocks.shape
    width = cur.shape[2]
    nrows = pick.shape[0]
    first = prev is None
    smem = pl.BlockSpec(memory_space=pltpu.SMEM)
    vmem = pl.BlockSpec(memory_space=pltpu.VMEM)
    anywhere = pl.BlockSpec(memory_space=pl.ANY)
    hbm = pltpu.MemorySpace.HBM
    if first:
        cur = pltpu.with_memory_space_constraint(cur, hbm)
    args = [
        pltpu.with_memory_space_constraint(columns, hbm), pick,
        pltpu.with_memory_space_constraint(scales, hbm), center, half_width, received, blocks, cur,
    ]
    in_specs = [anywhere, smem, anywhere, smem, smem, vmem, vmem, anywhere]
    if not first:
        args.append(prev)
        in_specs.append(vmem)
    flops = 2 * local_rows * per_row * orbitals * orbitals * width
    nbytes = blocks.size * 2 + 2 * received.size * 2 + 3 * cur.size * 2
    return pl.pallas_call(
        functools.partial(first_step_kernel, first),
        out_shape=(
            jax.ShapeDtypeStruct(cur.shape, jnp.bfloat16),
            jax.ShapeDtypeStruct((nrows, orbitals, width), jnp.bfloat16),
        ),
        in_specs=in_specs,
        out_specs=(vmem, vmem),
        scratch_shapes=[
            pltpu.SMEM(columns.shape, columns.dtype),
            pltpu.SMEM(scales.shape, scales.dtype),
            pltpu.VMEM(cur.shape, cur.dtype),
            pltpu.SemaphoreType.DMA((3,)),
        ],
        compiler_params=pltpu.CompilerParams(vmem_limit_bytes=8 * 1024 * 1024),
        cost_estimate=pl.CostEstimate(flops=flops, bytes_accessed=nbytes, transcendentals=0),
    )(*args)


def select_rows(panels, index):
    chosen = jnp.broadcast_to(panels[0][None], (index.shape[0],) + panels.shape[1:])
    for atom in range(1, panels.shape[0]):
        chosen = jnp.where((index == atom)[:, None, None], panels[atom][None], chosen)
    return chosen


def on_device(vectors, blocks, scales, columns, owners, center, half_width):
    nrows = lax.axis_size("rows")
    local_rows = blocks.shape[0]
    orbitals = blocks.shape[2]
    group_width = vectors.shape[1]
    asked = jnp.stack(
        [requests(columns, nrows, local_rows), requests(owners, nrows, local_rows)], axis=1
    )
    granted = lax.all_to_all(asked, "rows", split_axis=0, concat_axis=0, tiled=True)
    wanted = granted[:, 0]
    relay_want = granted[:, 1]

    def exchange(outgoing):
        return lax.all_to_all(outgoing, "rows", split_axis=0, concat_axis=0, tiled=True)

    blocks = pltpu.with_memory_space_constraint(blocks, pltpu.VMEM)
    previous = vectors.reshape(local_rows, orbitals, group_width)
    current, outgoing = first_chebyshev_step(
        columns, wanted, scales, center, half_width,
        exchange(select_rows(previous, wanted)), blocks, previous, None,
    )
    for step in range(1, STEPS):
        pick = relay_want if step == STEPS - 1 else wanted
        upcoming, outgoing = chebyshev_step(
            columns, pick, scales, center, half_width, exchange(outgoing), blocks, current, previous
        )
        previous, current = (current, upcoming)
    arrived = exchange(outgoing)
    placed = select_rows(arrived, owners // local_rows)
    return placed.reshape(local_rows * orbitals, group_width)


def solution(mesh):
    in_specs = (
        P("rows", "vecs"),
        P("rows", None, None, None),
        P("rows", None),
        P("rows", None),
        P("rows"),
        P(),
        P(),
    )
    out_specs = P("rows", "vecs")
    return jax.shard_map(
        on_device, mesh=mesh, in_specs=in_specs, out_specs=out_specs, check_vma=False
    )
```

```python
import functools

import jax
import jax.numpy as jnp
from jax import lax
from jax.experimental import pallas as pl
from jax.experimental.pallas import tpu as pltpu
from jax.sharding import PartitionSpec as P

STEPS = 4


def requests(index, nrows, local_rows):
    devices = jnp.arange(nrows, dtype=index.dtype).reshape((nrows,) + (1,) * index.ndim)
    hit = (index // local_rows)[None] == devices
    return jnp.max(jnp.where(hit, (index % local_rows)[None], 0), axis=tuple(range(1, index.ndim + 1)))


def step_kernel(first, cols_ref, pick_ref, scl_ref, c_ref, w_ref, recv_ref, blk_ref, cur_ref, *rest):
    if first:
        out_ref, go_ref = rest
    else:
        prev_ref, out_ref, go_ref = rest
    local_rows, per_row = cols_ref.shape
    shift = c_ref[0]
    width = w_ref[0]
    for r in range(local_rows):

        def body(k, acc):
            s = cols_ref[r, k] // local_rows
            prod = jnp.dot(blk_ref[r, k], recv_ref[s], preferred_element_type=jnp.float32)
            return acc + scl_ref[r, k] * prod

        acc = lax.fori_loop(
            0, per_row, body, jnp.zeros(out_ref.shape[1:], jnp.float32), unroll=True
        )
        cur = cur_ref[r].astype(jnp.float32)
        if first:
            new = (acc - shift * cur) / width
        else:
            new = 2.0 * (acc - shift * cur) / width - prev_ref[r].astype(jnp.float32)
        out_ref[r] = new.astype(out_ref.dtype)

    def put(e, carry):
        go_ref[e] = out_ref[pick_ref[e]]
        return carry

    lax.fori_loop(0, go_ref.shape[0], put, 0)


def first_step_kernel(first, cols_hbm, pick_ref, scl_hbm, c_ref, w_ref, recv_ref, blk_ref, cur_hbm, *rest):
    if first:
        out_ref, go_ref, cols_ref, scl_ref, cur_ref, sems = rest
    else:
        prev_ref, out_ref, go_ref, cols_ref, scl_ref, cur_ref, sems = rest
    copies = [
        pltpu.make_async_copy(cols_hbm, cols_ref, sems.at[0]),
        pltpu.make_async_copy(scl_hbm, scl_ref, sems.at[1]),
        pltpu.make_async_copy(cur_hbm, cur_ref, sems.at[2]),
    ]
    for copy in copies:
        copy.start()
    copies[0].wait()
    copies[1].wait()
    local_rows, per_row = cols_ref.shape
    shift = c_ref[0]
    width = w_ref[0]
    for r in range(local_rows):

        def body(k, acc):
            s = cols_ref[r, k] // local_rows
            prod = jnp.dot(blk_ref[r, k], recv_ref[s], preferred_element_type=jnp.float32)
            return acc + scl_ref[r, k] * prod

        acc = lax.fori_loop(
            0, per_row, body, jnp.zeros(out_ref.shape[1:], jnp.float32), unroll=True
        )
        if r == 0:
            copies[2].wait()
        cur = cur_ref[r].astype(jnp.float32)
        if first:
            new = (acc - shift * cur) / width
        else:
            new = 2.0 * (acc - shift * cur) / width - prev_ref[r].astype(jnp.float32)
        out_ref[r] = new.astype(out_ref.dtype)

    def put(e, carry):
        go_ref[e] = out_ref[pick_ref[e]]
        return carry

    lax.fori_loop(0, go_ref.shape[0], put, 0)


def chebyshev_step(columns, pick, scales, center, half_width, received, blocks, cur, prev):
    local_rows, per_row, orbitals, _ = blocks.shape
    width = cur.shape[2]
    nrows = pick.shape[0]
    first = prev is None
    smem = pl.BlockSpec(memory_space=pltpu.SMEM)
    vmem = pl.BlockSpec(memory_space=pltpu.VMEM)
    args = [columns, pick, scales, center, half_width, received, blocks, cur]
    if not first:
        args.append(prev)
    flops = 2 * local_rows * per_row * orbitals * orbitals * width
    nbytes = blocks.size * 2 + 2 * received.size * 2 + 3 * cur.size * 2
    return pl.pallas_call(
        functools.partial(step_kernel, first),
        out_shape=(
            jax.ShapeDtypeStruct(cur.shape, jnp.bfloat16),
            jax.ShapeDtypeStruct((nrows, orbitals, width), jnp.bfloat16),
        ),
        in_specs=[smem] * 5 + [vmem] * (len(args) - 5),
        out_specs=(vmem, vmem),
        compiler_params=pltpu.CompilerParams(vmem_limit_bytes=8 * 1024 * 1024),
        cost_estimate=pl.CostEstimate(flops=flops, bytes_accessed=nbytes, transcendentals=0),
    )(*args)


def first_chebyshev_step(columns, pick, scales, center, half_width, received, blocks, cur, prev):
    local_rows, per_row, orbitals, _ = blocks.shape
    width = cur.shape[2]
    nrows = pick.shape[0]
    first = prev is None
    smem = pl.BlockSpec(memory_space=pltpu.SMEM)
    vmem = pl.BlockSpec(memory_space=pltpu.VMEM)
    anywhere = pl.BlockSpec(memory_space=pl.ANY)
    hbm = pltpu.MemorySpace.HBM
    if first:
        cur = pltpu.with_memory_space_constraint(cur, hbm)
    args = [
        pltpu.with_memory_space_constraint(columns, hbm), pick,
        pltpu.with_memory_space_constraint(scales, hbm), center, half_width, received, blocks, cur,
    ]
    in_specs = [anywhere, smem, anywhere, smem, smem, vmem, vmem, anywhere]
    if not first:
        args.append(prev)
        in_specs.append(vmem)
    flops = 2 * local_rows * per_row * orbitals * orbitals * width
    nbytes = blocks.size * 2 + 2 * received.size * 2 + 3 * cur.size * 2
    return pl.pallas_call(
        functools.partial(first_step_kernel, first),
        out_shape=(
            jax.ShapeDtypeStruct(cur.shape, jnp.bfloat16),
            jax.ShapeDtypeStruct((nrows, orbitals, width), jnp.bfloat16),
        ),
        in_specs=in_specs,
        out_specs=(vmem, vmem),
        scratch_shapes=[
            pltpu.SMEM(columns.shape, columns.dtype),
            pltpu.SMEM(scales.shape, scales.dtype),
            pltpu.VMEM(cur.shape, cur.dtype),
            pltpu.SemaphoreType.DMA((3,)),
        ],
        compiler_params=pltpu.CompilerParams(vmem_limit_bytes=8 * 1024 * 1024),
        cost_estimate=pl.CostEstimate(flops=flops, bytes_accessed=nbytes, transcendentals=0),
    )(*args)


def select_rows(panels, index):
    chosen = jnp.broadcast_to(panels[0][None], (index.shape[0],) + panels.shape[1:])
    for atom in range(1, panels.shape[0]):
        chosen = jnp.where((index == atom)[:, None, None], panels[atom][None], chosen)
    return chosen


def on_device(vectors, blocks, scales, columns, owners, center, half_width):
    nrows = lax.axis_size("rows")
    local_rows = blocks.shape[0]
    orbitals = blocks.shape[2]
    group_width = vectors.shape[1]
    lane = lax.broadcasted_iota(jnp.int32, (nrows, 128), 1)
    asked = jnp.where(
        lane == 0,
        requests(columns, nrows, local_rows)[:, None],
        jnp.where(lane == 1, requests(owners, nrows, local_rows)[:, None], 0),
    )
    granted = lax.all_to_all(asked, "rows", split_axis=0, concat_axis=0, tiled=True)
    wanted = granted[:, 0]
    relay_want = granted[:, 1]

    def exchange(outgoing):
        return lax.all_to_all(outgoing, "rows", split_axis=0, concat_axis=0, tiled=True)

    blocks = pltpu.with_memory_space_constraint(blocks, pltpu.VMEM)
    previous = vectors.reshape(local_rows, orbitals, group_width)
    current, outgoing = first_chebyshev_step(
        columns, wanted, scales, center, half_width,
        exchange(select_rows(previous, wanted)), blocks, previous, None,
    )
    for step in range(1, STEPS):
        pick = relay_want if step == STEPS - 1 else wanted
        upcoming, outgoing = chebyshev_step(
            columns, pick, scales, center, half_width, exchange(outgoing), blocks, current, previous
        )
        previous, current = (current, upcoming)
    arrived = exchange(outgoing)
    placed = jnp.take(arrived, owners // local_rows, axis=0, mode="clip")
    return placed.reshape(local_rows * orbitals, group_width)


def solution(mesh):
    in_specs = (
        P("rows", "vecs"),
        P("rows", None, None, None),
        P("rows", None),
        P("rows", None),
        P("rows"),
        P(),
        P(),
    )
    out_specs = P("rows", "vecs")
    return jax.shard_map(
        on_device, mesh=mesh, in_specs=in_specs, out_specs=out_specs, check_vma=False
    )
```

```python
import functools

import jax
import jax.numpy as jnp
from jax import lax
from jax.experimental import pallas as pl
from jax.experimental.pallas import tpu as pltpu
from jax.sharding import PartitionSpec as P

STEPS = 4


def requests(index, nrows, local_rows):
    devices = jnp.arange(nrows, dtype=index.dtype).reshape((nrows,) + (1,) * index.ndim)
    hit = (index // local_rows)[None] == devices
    return jnp.max(jnp.where(hit, (index % local_rows)[None], 0), axis=tuple(range(1, index.ndim + 1)))


def step_kernel(first, last, cols_ref, pick_ref, scl_ref, c_ref, w_ref, recv_ref, blk_ref, cur_ref, *rest):
    if first:
        out_ref, go_ref = rest
    elif last:
        prev_ref, go_ref, out_ref = rest
    else:
        prev_ref, out_ref, go_ref = rest
    local_rows, per_row = cols_ref.shape
    shift = c_ref[0]
    width = w_ref[0]
    for r in range(local_rows):

        def body(k, acc):
            s = cols_ref[r, k] // local_rows
            prod = jnp.dot(blk_ref[r, k], recv_ref[s], preferred_element_type=jnp.float32)
            return acc + scl_ref[r, k] * prod

        acc = lax.fori_loop(
            0, per_row, body, jnp.zeros(out_ref.shape[1:], jnp.float32), unroll=True
        )
        cur = cur_ref[r].astype(jnp.float32)
        if first:
            new = (acc - shift * cur) / width
        else:
            new = 2.0 * (acc - shift * cur) / width - prev_ref[r].astype(jnp.float32)
        out_ref[r] = new.astype(out_ref.dtype)

    def put(e, carry):
        go_ref[e] = out_ref[pick_ref[e]]
        return carry

    lax.fori_loop(0, go_ref.shape[0], put, 0)


def first_step_kernel(first, cols_hbm, pick_ref, scl_hbm, c_ref, w_ref, recv_ref, blk_ref, cur_hbm, *rest):
    if first:
        out_ref, go_ref, cols_ref, scl_ref, cur_ref, sems = rest
    else:
        prev_ref, out_ref, go_ref, cols_ref, scl_ref, cur_ref, sems = rest
    copies = [
        pltpu.make_async_copy(cols_hbm, cols_ref, sems.at[0]),
        pltpu.make_async_copy(scl_hbm, scl_ref, sems.at[1]),
        pltpu.make_async_copy(cur_hbm, cur_ref, sems.at[2]),
    ]
    for copy in copies:
        copy.start()
    copies[0].wait()
    copies[1].wait()
    local_rows, per_row = cols_ref.shape
    shift = c_ref[0]
    width = w_ref[0]
    for r in range(local_rows):

        def body(k, acc):
            s = cols_ref[r, k] // local_rows
            prod = jnp.dot(blk_ref[r, k], recv_ref[s], preferred_element_type=jnp.float32)
            return acc + scl_ref[r, k] * prod

        acc = lax.fori_loop(
            0, per_row, body, jnp.zeros(out_ref.shape[1:], jnp.float32), unroll=True
        )
        if r == 0:
            copies[2].wait()
        cur = cur_ref[r].astype(jnp.float32)
        if first:
            new = (acc - shift * cur) / width
        else:
            new = 2.0 * (acc - shift * cur) / width - prev_ref[r].astype(jnp.float32)
        out_ref[r] = new.astype(out_ref.dtype)

    def put(e, carry):
        go_ref[e] = out_ref[pick_ref[e]]
        return carry

    lax.fori_loop(0, go_ref.shape[0], put, 0)


def chebyshev_step(columns, pick, scales, center, half_width, received, blocks, cur, prev, last=False):
    local_rows, per_row, orbitals, _ = blocks.shape
    width = cur.shape[2]
    nrows = pick.shape[0]
    first = prev is None
    smem = pl.BlockSpec(memory_space=pltpu.SMEM)
    vmem = pl.BlockSpec(memory_space=pltpu.VMEM)
    args = [columns, pick, scales, center, half_width, received, blocks, cur]
    if not first:
        args.append(prev)
    flops = 2 * local_rows * per_row * orbitals * orbitals * width
    nbytes = blocks.size * 2 + 2 * received.size * 2 + 3 * cur.size * 2
    return pl.pallas_call(
        functools.partial(step_kernel, first, last),
        out_shape=(
            (jax.ShapeDtypeStruct((nrows, orbitals, width), jnp.bfloat16),)
            if last
            else (
                jax.ShapeDtypeStruct(cur.shape, jnp.bfloat16),
                jax.ShapeDtypeStruct((nrows, orbitals, width), jnp.bfloat16),
            )
        ),
        in_specs=[smem] * 5 + [vmem] * (len(args) - 5),
        out_specs=(vmem,) if last else (vmem, vmem),
        scratch_shapes=[pltpu.VMEM(cur.shape, jnp.bfloat16)] if last else [],
        compiler_params=pltpu.CompilerParams(vmem_limit_bytes=8 * 1024 * 1024),
        cost_estimate=pl.CostEstimate(flops=flops, bytes_accessed=nbytes, transcendentals=0),
    )(*args)


def first_chebyshev_step(columns, pick, scales, center, half_width, received, blocks, cur, prev):
    local_rows, per_row, orbitals, _ = blocks.shape
    width = cur.shape[2]
    nrows = pick.shape[0]
    first = prev is None
    smem = pl.BlockSpec(memory_space=pltpu.SMEM)
    vmem = pl.BlockSpec(memory_space=pltpu.VMEM)
    anywhere = pl.BlockSpec(memory_space=pl.ANY)
    hbm = pltpu.MemorySpace.HBM
    if first:
        cur = pltpu.with_memory_space_constraint(cur, hbm)
    args = [
        pltpu.with_memory_space_constraint(columns, hbm), pick,
        pltpu.with_memory_space_constraint(scales, hbm), center, half_width, received, blocks, cur,
    ]
    in_specs = [anywhere, smem, anywhere, smem, smem, vmem, vmem, anywhere]
    if not first:
        args.append(prev)
        in_specs.append(vmem)
    flops = 2 * local_rows * per_row * orbitals * orbitals * width
    nbytes = blocks.size * 2 + 2 * received.size * 2 + 3 * cur.size * 2
    return pl.pallas_call(
        functools.partial(first_step_kernel, first),
        out_shape=(
            jax.ShapeDtypeStruct(cur.shape, jnp.bfloat16),
            jax.ShapeDtypeStruct((nrows, orbitals, width), jnp.bfloat16),
        ),
        in_specs=in_specs,
        out_specs=(vmem, vmem),
        scratch_shapes=[
            pltpu.SMEM(columns.shape, columns.dtype),
            pltpu.SMEM(scales.shape, scales.dtype),
            pltpu.VMEM(cur.shape, cur.dtype),
            pltpu.SemaphoreType.DMA((3,)),
        ],
        compiler_params=pltpu.CompilerParams(vmem_limit_bytes=8 * 1024 * 1024),
        cost_estimate=pl.CostEstimate(flops=flops, bytes_accessed=nbytes, transcendentals=0),
    )(*args)


def select_rows(panels, index):
    chosen = jnp.broadcast_to(panels[0][None], (index.shape[0],) + panels.shape[1:])
    for atom in range(1, panels.shape[0]):
        chosen = jnp.where((index == atom)[:, None, None], panels[atom][None], chosen)
    return chosen


def on_device(vectors, blocks, scales, columns, owners, center, half_width):
    nrows = lax.axis_size("rows")
    local_rows = blocks.shape[0]
    orbitals = blocks.shape[2]
    group_width = vectors.shape[1]
    asked = jnp.stack(
        [requests(columns, nrows, local_rows), requests(owners, nrows, local_rows)], axis=1
    )
    granted = lax.all_to_all(asked, "rows", split_axis=0, concat_axis=0, tiled=True)
    wanted = granted[:, 0]
    relay_want = granted[:, 1]

    def exchange(outgoing):
        return lax.all_to_all(outgoing, "rows", split_axis=0, concat_axis=0, tiled=True)

    blocks = pltpu.with_memory_space_constraint(blocks, pltpu.VMEM)
    previous = vectors.reshape(local_rows, orbitals, group_width)
    current, outgoing = first_chebyshev_step(
        columns, wanted, scales, center, half_width,
        exchange(select_rows(previous, wanted)), blocks, previous, None,
    )
    for step in range(1, STEPS - 1):
        upcoming, outgoing = chebyshev_step(
            columns, wanted, scales, center, half_width, exchange(outgoing), blocks, current, previous
        )
        previous, current = (current, upcoming)
    (outgoing,) = chebyshev_step(
        columns, relay_want, scales, center, half_width, exchange(outgoing), blocks, current,
        previous, last=True,
    )
    arrived = exchange(outgoing)
    placed = jnp.take(arrived, owners // local_rows, axis=0, mode="clip")
    return placed.reshape(local_rows * orbitals, group_width)


def solution(mesh):
    in_specs = (
        P("rows", "vecs"),
        P("rows", None, None, None),
        P("rows", None),
        P("rows", None),
        P("rows"),
        P(),
        P(),
    )
    out_specs = P("rows", "vecs")
    return jax.shard_map(
        on_device, mesh=mesh, in_specs=in_specs, out_specs=out_specs, check_vma=False
    )
```

```python
import functools

import jax
import jax.numpy as jnp
from jax import lax
from jax.experimental import pallas as pl
from jax.experimental.pallas import tpu as pltpu
from jax.sharding import PartitionSpec as P

STEPS = 4


def requests(index, nrows, local_rows):
    devices = jnp.arange(nrows, dtype=index.dtype).reshape((nrows,) + (1,) * index.ndim)
    hit = (index // local_rows)[None] == devices
    return jnp.max(jnp.where(hit, (index % local_rows)[None], 0), axis=tuple(range(1, index.ndim + 1)))


def step_kernel(first, cols_ref, pick_ref, scl_ref, c_ref, w_ref, recv_ref, blk_ref, cur_ref, *rest):
    if first:
        out_ref, go_ref = rest
    else:
        prev_ref, out_ref, go_ref = rest
    local_rows, per_row = cols_ref.shape
    shift = c_ref[0]
    width = w_ref[0]
    for r in range(local_rows):

        def body(k, acc):
            s = cols_ref[r, k] // local_rows
            prod = jnp.dot(blk_ref[r, k], recv_ref[s], preferred_element_type=jnp.float32)
            return acc + scl_ref[r, k] * prod

        acc = lax.fori_loop(
            0, per_row, body, jnp.zeros(out_ref.shape[1:], jnp.float32), unroll=True
        )
        cur = cur_ref[r].astype(jnp.float32)
        if first:
            new = (acc - shift * cur) / width
        else:
            new = 2.0 * (acc - shift * cur) / width - prev_ref[r].astype(jnp.float32)
        out_ref[r] = new.astype(out_ref.dtype)

    def put(e, carry):
        go_ref[e] = out_ref[pick_ref[e]]
        return carry

    lax.fori_loop(0, go_ref.shape[0], put, 0)


def first_step_kernel(first, slot_ref, pick_ref, scl_ref, c_ref, w_ref, recv_ref, blk_ref, cur_hbm, *rest):
    if first:
        out_ref, go_ref, cur_ref, sems = rest
    else:
        prev_ref, out_ref, go_ref, cur_ref, sems = rest
    copy = pltpu.make_async_copy(cur_hbm, cur_ref, sems.at[0])
    copy.start()
    local_rows, per_row = slot_ref.shape
    shift = c_ref[0]
    width = w_ref[0]
    for r in range(local_rows):

        def body(k, acc):
            s = slot_ref[r, k]
            prod = jnp.dot(blk_ref[r, k], recv_ref[s], preferred_element_type=jnp.float32)
            return acc + scl_ref[r, k] * prod

        acc = lax.fori_loop(
            0, per_row, body, jnp.zeros(out_ref.shape[1:], jnp.float32), unroll=True
        )
        if r == 0:
            copy.wait()
        cur = cur_ref[r].astype(jnp.float32)
        if first:
            new = (acc - shift * cur) / width
        else:
            new = 2.0 * (acc - shift * cur) / width - prev_ref[r].astype(jnp.float32)
        out_ref[r] = new.astype(out_ref.dtype)

    def put(e, carry):
        go_ref[e] = out_ref[pick_ref[e]]
        return carry

    lax.fori_loop(0, go_ref.shape[0], put, 0)


def chebyshev_step(columns, pick, scales, center, half_width, received, blocks, cur, prev):
    local_rows, per_row, orbitals, _ = blocks.shape
    width = cur.shape[2]
    nrows = pick.shape[0]
    first = prev is None
    smem = pl.BlockSpec(memory_space=pltpu.SMEM)
    vmem = pl.BlockSpec(memory_space=pltpu.VMEM)
    args = [columns, pick, scales, center, half_width, received, blocks, cur]
    if not first:
        args.append(prev)
    flops = 2 * local_rows * per_row * orbitals * orbitals * width
    nbytes = blocks.size * 2 + 2 * received.size * 2 + 3 * cur.size * 2
    return pl.pallas_call(
        functools.partial(step_kernel, first),
        out_shape=(
            jax.ShapeDtypeStruct(cur.shape, jnp.bfloat16),
            jax.ShapeDtypeStruct((nrows, orbitals, width), jnp.bfloat16),
        ),
        in_specs=[smem] * 5 + [vmem] * (len(args) - 5),
        out_specs=(vmem, vmem),
        compiler_params=pltpu.CompilerParams(vmem_limit_bytes=8 * 1024 * 1024),
        cost_estimate=pl.CostEstimate(flops=flops, bytes_accessed=nbytes, transcendentals=0),
    )(*args)


def first_chebyshev_step(columns, pick, scales, center, half_width, received, blocks, cur, prev):
    local_rows, per_row, orbitals, _ = blocks.shape
    width = cur.shape[2]
    nrows = pick.shape[0]
    first = prev is None
    smem = pl.BlockSpec(memory_space=pltpu.SMEM)
    vmem = pl.BlockSpec(memory_space=pltpu.VMEM)
    anywhere = pl.BlockSpec(memory_space=pl.ANY)
    hbm = pltpu.MemorySpace.HBM
    if first:
        cur = pltpu.with_memory_space_constraint(cur, hbm)
    args = [
        columns // blocks.shape[0], pick, scales + 0.0, center, half_width, received, blocks, cur,
    ]
    in_specs = [smem, smem, smem, smem, smem, vmem, vmem, anywhere]
    if not first:
        args.append(prev)
        in_specs.append(vmem)
    flops = 2 * local_rows * per_row * orbitals * orbitals * width
    nbytes = blocks.size * 2 + 2 * received.size * 2 + 3 * cur.size * 2
    return pl.pallas_call(
        functools.partial(first_step_kernel, first),
        out_shape=(
            jax.ShapeDtypeStruct(cur.shape, jnp.bfloat16),
            jax.ShapeDtypeStruct((nrows, orbitals, width), jnp.bfloat16),
        ),
        in_specs=in_specs,
        out_specs=(vmem, vmem),
        scratch_shapes=[
            pltpu.VMEM(cur.shape, cur.dtype),
            pltpu.SemaphoreType.DMA((1,)),
        ],
        compiler_params=pltpu.CompilerParams(vmem_limit_bytes=8 * 1024 * 1024),
        cost_estimate=pl.CostEstimate(flops=flops, bytes_accessed=nbytes, transcendentals=0),
    )(*args)


def select_rows(panels, index):
    chosen = jnp.broadcast_to(panels[0][None], (index.shape[0],) + panels.shape[1:])
    for atom in range(1, panels.shape[0]):
        chosen = jnp.where((index == atom)[:, None, None], panels[atom][None], chosen)
    return chosen


def on_device(vectors, blocks, scales, columns, owners, center, half_width):
    nrows = lax.axis_size("rows")
    local_rows = blocks.shape[0]
    orbitals = blocks.shape[2]
    group_width = vectors.shape[1]
    asked = jnp.stack(
        [requests(columns, nrows, local_rows), requests(owners, nrows, local_rows)], axis=1
    )
    granted = lax.all_to_all(asked, "rows", split_axis=0, concat_axis=0, tiled=True)
    wanted = granted[:, 0]
    relay_want = granted[:, 1]

    def exchange(outgoing):
        return lax.all_to_all(outgoing, "rows", split_axis=0, concat_axis=0, tiled=True)

    blocks = pltpu.with_memory_space_constraint(blocks, pltpu.VMEM)
    previous = vectors.reshape(local_rows, orbitals, group_width)
    current, outgoing = first_chebyshev_step(
        columns, wanted, scales, center, half_width,
        exchange(select_rows(previous, wanted)), blocks, previous, None,
    )
    for step in range(1, STEPS):
        pick = relay_want if step == STEPS - 1 else wanted
        upcoming, outgoing = chebyshev_step(
            columns, pick, scales, center, half_width, exchange(outgoing), blocks, current, previous
        )
        previous, current = (current, upcoming)
    arrived = exchange(outgoing)
    placed = jnp.take(arrived, owners // local_rows, axis=0, mode="clip")
    return placed.reshape(local_rows * orbitals, group_width)


def solution(mesh):
    in_specs = (
        P("rows", "vecs"),
        P("rows", None, None, None),
        P("rows", None),
        P("rows", None),
        P("rows"),
        P(),
        P(),
    )
    out_specs = P("rows", "vecs")
    return jax.shard_map(
        on_device, mesh=mesh, in_specs=in_specs, out_specs=out_specs, check_vma=False
    )
```

```python
import functools

import jax
import jax.numpy as jnp
from jax import lax
from jax.experimental import pallas as pl
from jax.experimental.pallas import tpu as pltpu
from jax.sharding import PartitionSpec as P

STEPS = 4


def requests(index, nrows, local_rows):
    devices = jnp.arange(nrows, dtype=index.dtype).reshape((nrows,) + (1,) * index.ndim)
    hit = (index // local_rows)[None] == devices
    return jnp.max(jnp.where(hit, (index % local_rows)[None], 0), axis=tuple(range(1, index.ndim + 1)))


def step_kernel(first, cols_ref, pick_ref, scl_ref, c_ref, w_ref, recv_ref, blk_ref, cur_ref, *rest):
    if first:
        out_ref, go_ref = rest
    else:
        prev_ref, out_ref, go_ref = rest
    local_rows, per_row = cols_ref.shape
    shift = c_ref[0]
    width = w_ref[0]
    for r in range(local_rows):

        def body(k, acc):
            s = cols_ref[r, k] // local_rows
            prod = jnp.dot(blk_ref[r, k], recv_ref[s], preferred_element_type=jnp.float32)
            return acc + scl_ref[r, k] * prod

        acc = lax.fori_loop(
            0, per_row, body, jnp.zeros(out_ref.shape[1:], jnp.float32), unroll=True
        )
        cur = cur_ref[r].astype(jnp.float32)
        if first:
            new = (acc - shift * cur) / width
        else:
            new = 2.0 * (acc - shift * cur) / width - prev_ref[r].astype(jnp.float32)
        out_ref[r] = new.astype(out_ref.dtype)

    def put(e, carry):
        go_ref[e] = out_ref[pick_ref[e]]
        return carry

    lax.fori_loop(0, go_ref.shape[0], put, 0)


def first_step_kernel(first, slot_ref, pick_ref, scl_ref, c_ref, w_ref, recv_ref, blk_ref, cur_hbm, *rest):
    if first:
        out_ref, go_ref, cur_ref, sems = rest
    else:
        prev_ref, out_ref, go_ref, cur_ref, sems = rest
    copy = pltpu.make_async_copy(cur_hbm, cur_ref, sems.at[0])
    copy.start()
    local_rows, per_row = slot_ref.shape
    shift = c_ref[0]
    width = w_ref[0]
    for r in range(local_rows):

        def body(k, acc):
            s = slot_ref[r, k]
            prod = jnp.dot(blk_ref[r, k], recv_ref[s], preferred_element_type=jnp.float32)
            return acc + scl_ref[r, k] * prod

        acc = lax.fori_loop(
            0, per_row, body, jnp.zeros(out_ref.shape[1:], jnp.float32), unroll=True
        )
        if r == 0:
            copy.wait()
        cur = cur_ref[r].astype(jnp.float32)
        if first:
            new = (acc - shift * cur) / width
        else:
            new = 2.0 * (acc - shift * cur) / width - prev_ref[r].astype(jnp.float32)
        out_ref[r] = new.astype(out_ref.dtype)

    def put(e, carry):
        go_ref[e] = out_ref[pick_ref[e]]
        return carry

    lax.fori_loop(0, go_ref.shape[0], put, 0)


def chebyshev_step(columns, pick, scales, center, half_width, received, blocks, cur, prev):
    local_rows, per_row, orbitals, _ = blocks.shape
    width = cur.shape[2]
    nrows = pick.shape[0]
    first = prev is None
    smem = pl.BlockSpec(memory_space=pltpu.SMEM)
    vmem = pl.BlockSpec(memory_space=pltpu.VMEM)
    args = [columns, pick, scales, center, half_width, received, blocks, cur]
    if not first:
        args.append(prev)
    flops = 2 * local_rows * per_row * orbitals * orbitals * width
    nbytes = blocks.size * 2 + 2 * received.size * 2 + 3 * cur.size * 2
    return pl.pallas_call(
        functools.partial(step_kernel, first),
        out_shape=(
            jax.ShapeDtypeStruct(cur.shape, jnp.bfloat16),
            jax.ShapeDtypeStruct((nrows, orbitals, width), jnp.bfloat16),
        ),
        in_specs=[smem] * 5 + [vmem] * (len(args) - 5),
        out_specs=(vmem, vmem),
        compiler_params=pltpu.CompilerParams(vmem_limit_bytes=8 * 1024 * 1024),
        cost_estimate=pl.CostEstimate(flops=flops, bytes_accessed=nbytes, transcendentals=0),
    )(*args)


def first_chebyshev_step(columns, pick, scales, center, half_width, received, blocks, cur, prev):
    local_rows, per_row, orbitals, _ = blocks.shape
    width = cur.shape[2]
    nrows = pick.shape[0]
    first = prev is None
    smem = pl.BlockSpec(memory_space=pltpu.SMEM)
    vmem = pl.BlockSpec(memory_space=pltpu.VMEM)
    anywhere = pl.BlockSpec(memory_space=pl.ANY)
    hbm = pltpu.MemorySpace.HBM
    if first:
        cur = pltpu.with_memory_space_constraint(cur, hbm)
    args = [
        columns // blocks.shape[0], pick, jnp.abs(scales), center, half_width, received, blocks, cur,
    ]
    in_specs = [smem, smem, smem, smem, smem, vmem, vmem, anywhere]
    if not first:
        args.append(prev)
        in_specs.append(vmem)
    flops = 2 * local_rows * per_row * orbitals * orbitals * width
    nbytes = blocks.size * 2 + 2 * received.size * 2 + 3 * cur.size * 2
    return pl.pallas_call(
        functools.partial(first_step_kernel, first),
        out_shape=(
            jax.ShapeDtypeStruct(cur.shape, jnp.bfloat16),
            jax.ShapeDtypeStruct((nrows, orbitals, width), jnp.bfloat16),
        ),
        in_specs=in_specs,
        out_specs=(vmem, vmem),
        scratch_shapes=[
            pltpu.VMEM(cur.shape, cur.dtype),
            pltpu.SemaphoreType.DMA((1,)),
        ],
        compiler_params=pltpu.CompilerParams(vmem_limit_bytes=8 * 1024 * 1024),
        cost_estimate=pl.CostEstimate(flops=flops, bytes_accessed=nbytes, transcendentals=0),
    )(*args)


def select_rows(panels, index):
    chosen = jnp.broadcast_to(panels[0][None], (index.shape[0],) + panels.shape[1:])
    for atom in range(1, panels.shape[0]):
        chosen = jnp.where((index == atom)[:, None, None], panels[atom][None], chosen)
    return chosen


def on_device(vectors, blocks, scales, columns, owners, center, half_width):
    nrows = lax.axis_size("rows")
    local_rows = blocks.shape[0]
    orbitals = blocks.shape[2]
    group_width = vectors.shape[1]
    asked = jnp.stack(
        [requests(columns, nrows, local_rows), requests(owners, nrows, local_rows)], axis=1
    )
    granted = lax.all_to_all(asked, "rows", split_axis=0, concat_axis=0, tiled=True)
    wanted = granted[:, 0]
    relay_want = granted[:, 1]

    def exchange(outgoing):
        return lax.all_to_all(outgoing, "rows", split_axis=0, concat_axis=0, tiled=True)

    blocks = pltpu.with_memory_space_constraint(blocks, pltpu.VMEM)
    previous = vectors.reshape(local_rows, orbitals, group_width)
    current, outgoing = first_chebyshev_step(
        columns, wanted, scales, center, half_width,
        exchange(select_rows(previous, wanted)), blocks, previous, None,
    )
    for step in range(1, STEPS):
        pick = relay_want if step == STEPS - 1 else wanted
        upcoming, outgoing = chebyshev_step(
            columns, pick, scales, center, half_width, exchange(outgoing), blocks, current, previous
        )
        previous, current = (current, upcoming)
    arrived = exchange(outgoing)
    placed = jnp.take(arrived, owners // local_rows, axis=0, mode="clip")
    return placed.reshape(local_rows * orbitals, group_width)


def solution(mesh):
    in_specs = (
        P("rows", "vecs"),
        P("rows", None, None, None),
        P("rows", None),
        P("rows", None),
        P("rows"),
        P(),
        P(),
    )
    out_specs = P("rows", "vecs")
    return jax.shard_map(
        on_device, mesh=mesh, in_specs=in_specs, out_specs=out_specs, check_vma=False
    )
```
